512 devices in a mesh: segment: 16 (over y, z_lo), ctx: 32 (over x, z_hi, core).
Axes of the slice: x: 4, y: 8, z: 8 (z_hi: 4, z_lo: 2; z = z_hi * 2 + z_lo), core: 2. Of those that a mesh axis runs over, the one named last changes fastest.
Arguments:
- perturbed_frame_activation: bfloat16 [2, 256, 1536], P(None, 'ctx'), may hold values from -8 to 8
- inbound_activation: bfloat16 [16, 256, 1536], P('segment', 'ctx'), may hold values from -6 to 6
- section_block_indices: int32 [16], P('segment'), may hold values from 1 to 2, as said below
- tile_arrival_permutation: int32 [2], replicated, may hold values from 0 to 1, each once
- adaptive_shifting: float32 [16, 2, 1536], P('segment'), may hold values from -6 to 6
- adaptive_scaling: float32 [16, 2, 1536], P('segment'), may hold values from -4 to 4
- tier_query_factor: float32 [16, 2, 1536], P('segment'), may hold values from 0.3 to 3
- tier_skip_coefficient: float32 [16, 2, 1536], P('segment'), may hold values from -12 to 12
- earlier_step_lookup_matrix: bfloat16 [16, 2, 2, 256, 1536], P('segment', None, None, 'ctx'), may hold values from -10.5 to 10.5
- earlier_step_content_matrix: bfloat16 [16, 2, 2, 256, 1536], P('segment', None, None, 'ctx'), may hold values from -3 to 3
Outputs:
- section_out: bfloat16 [16, 2, 256, 1536], P('segment', None, 'ctx')
The draws below stay inside these ranges and needn't reach their ends.
Inputs may be any that keep to these rules, and one draw needn't show every extreme that they name: `section_block_indices`: some segment uses exactly 2 slots and some exactly 1. `tile_arrival_permutation`: each patch once.
All inputs are finite; a program needn't handle non-finite values.
Results may differ from the reference program's by a relative error of at most 0.013.
Values may be sent and summed in bfloat16 or wider, within the bound.
No kernel may reach another device: no remote copies, remote signals or barrier semaphores. Data moves between devices by JAX's collectives and lax.ppermute only.
A program may use at most 64 MiB of HBM per device.

```python
import math
import jax
import jax.numpy as jnp
from jax import lax

HEADS = 12
HD = 128
PATCHES = 2
LMAX = 2
EMBED_WIDTH = 1536
PIECE_ELEMENTS = 256
TOKENS = 512
N_SEGMENT = 16


def draw_perturbed_frame_activation(key, part):
    key_base, key_rows, key_cols = jax.random.split(key, 3)
    array_shape = (PATCHES, PIECE_ELEMENTS, EMBED_WIDTH)
    base = jax.random.normal(key_base, array_shape, jnp.float32)
    row_scale = jnp.exp(jax.random.uniform(key_rows, (PATCHES, PIECE_ELEMENTS, 1), jnp.float32, 0.0, 1.4))
    col_scale = jnp.exp(jax.random.uniform(key_cols, (1, 1, EMBED_WIDTH), jnp.float32, -1.2, 1.2))
    return jnp.clip(0.5 * base * row_scale * col_scale, -8.0, 8.0).astype(jnp.bfloat16)


def draw_section_block_indices(key, part):
    key_counts, key_places = jax.random.split(jax.random.fold_in(key, 7), 2)
    counts = jax.random.randint(key_counts, (N_SEGMENT,), 1, LMAX + 1)
    places = jax.random.permutation(key_places, N_SEGMENT)
    counts = counts.at[places[0]].set(LMAX)
    counts = counts.at[places[1]].set(1)
    return counts.astype(jnp.int32)


def draw_earlier_step_lookup_matrix(key, part):
    key_base, key_rows = jax.random.split(jax.random.fold_in(key, 11), 2)
    array_shape = (N_SEGMENT, LMAX, PATCHES, PIECE_ELEMENTS, EMBED_WIDTH)
    base = jnp.clip(jax.random.normal(key_base, array_shape, jnp.float32), -3.0, 3.0)
    row_scale = jnp.exp(jax.random.uniform(key_rows, (N_SEGMENT, LMAX, PATCHES, PIECE_ELEMENTS, 1), jnp.float32, 0.0, 1.25))
    return (base * row_scale).astype(jnp.bfloat16)


def block_levels(own_key, extent, shards, low, top_value):
    def one(dim, blocks):
        draws = jax.random.uniform(jax.random.fold_in(jax.random.fold_in(own_key, 6), dim), (blocks,), jnp.float32, low / len(shards), top_value / len(shards))
        return jnp.repeat(jnp.exp(draws), extent[dim] // blocks).reshape((-1,) + (1,) * (len(extent) - dim - 1))

    factor_of = one(*shards[0])
    for cut in shards[1:]:
        factor_of = factor_of * one(*cut)
    return factor_of


def gaussian(own_key, shape, scale, most, shards=(), kind=jnp.bfloat16):
    entries = jax.random.normal(own_key, shape, jnp.float32) * scale
    if len(shards) > 0:
        entries = block_levels(own_key, shape, shards, -0.22, 0.18) * entries
    return jnp.clip(entries, min=-most, max=most).astype(kind)


def setup_inputs(seed: int = 0) -> dict:
    key_list = jax.random.split(jax.random.key(seed), 11)
    return {
        "perturbed_frame_activation": draw_perturbed_frame_activation(jax.random.fold_in(key_list[10], 71), 0),
        "inbound_activation": gaussian(key_list[1], (N_SEGMENT, PIECE_ELEMENTS, EMBED_WIDTH), 1.0, 6.0, ((0, 16), (1, 32))),
        "section_block_indices": draw_section_block_indices(jax.random.fold_in(key_list[10], 71), 0),
        "tile_arrival_permutation": jax.random.permutation(key_list[3], PATCHES).astype(jnp.int32),
        "adaptive_shifting": gaussian(key_list[4], (N_SEGMENT, LMAX, EMBED_WIDTH), 0.5, 6.0, ((0, 16),), jnp.float32),
        "adaptive_scaling": gaussian(key_list[5], (N_SEGMENT, LMAX, EMBED_WIDTH), 0.3, 4.0, ((0, 16),), jnp.float32),
        "tier_query_factor": jnp.clip(jnp.exp(math.log(3.0) - 2.3025851 * jax.random.uniform(key_list[6], (N_SEGMENT, LMAX, EMBED_WIDTH), jnp.float32) ** block_levels(key_list[6], (N_SEGMENT, LMAX, EMBED_WIDTH), ((0, 16),), -0.2, 0.2)), 0.3, 3.0),
        "tier_skip_coefficient": gaussian(key_list[7], (N_SEGMENT, LMAX, EMBED_WIDTH), 2.0, 12.0, ((0, 16),), jnp.float32),
        "earlier_step_lookup_matrix": draw_earlier_step_lookup_matrix(jax.random.fold_in(key_list[10], 71), 0),
        "earlier_step_content_matrix": gaussian(key_list[9], (N_SEGMENT, LMAX, PATCHES, PIECE_ELEMENTS, EMBED_WIDTH), 1.0, 3.0, ((0, 16), (3, 32))),
    }


EPSILON = 1e-06

def head_norm(values):
    return values * lax.rsqrt(lax.optimization_barrier(jnp.mean(values * values, axis=-1, keepdims=True)) + EPSILON)

def transform_level(passing_vessel, displacement_line, stretch_line, probe_factor_line, skip_coefficient_line, cached_probe_vectors, cached_payload_vectors, tile_number):
    activation_single_precision = passing_vessel.astype(jnp.float32)
    hidden = activation_single_precision * lax.rsqrt(lax.optimization_barrier(jnp.mean(activation_single_precision * activation_single_precision, axis=-1, keepdims=True)) + EPSILON) * (1.0 + stretch_line) + displacement_line
    query_heads = head_norm(hidden.reshape(PIECE_ELEMENTS, HEADS, HD)).astype(jnp.bfloat16)
    fresh_key = head_norm((hidden * probe_factor_line).reshape(PIECE_ELEMENTS, HEADS, HD)).reshape(PIECE_ELEMENTS, HEADS * HD).astype(jnp.bfloat16)
    fresh_value = hidden.astype(jnp.bfloat16)
    zero_index = jnp.zeros((), jnp.int32)
    position = (tile_number.astype(jnp.int32), zero_index, zero_index)
    cached_probe_vectors = lax.dynamic_update_slice(cached_probe_vectors, fresh_key[None], position)
    cached_payload_vectors = lax.dynamic_update_slice(cached_payload_vectors, fresh_value[None], position)
    all_keys = cached_probe_vectors.reshape(TOKENS, HEADS, HD).astype(jnp.float32)
    all_values = cached_payload_vectors.reshape(TOKENS, HEADS, HD).astype(jnp.float32)
    scores = jnp.einsum('phd,nhd->phn', query_heads.astype(jnp.float32), all_keys) * (1.0 / math.sqrt(HD))
    weights = jnp.exp(scores)
    softmax_total = lax.optimization_barrier(jnp.sum(weights, axis=-1))
    rounded_weights = lax.optimization_barrier(weights.astype(jnp.bfloat16)).astype(jnp.float32)
    numerator = jnp.einsum('phn,nhd->phd', rounded_weights, all_values)
    attended = (numerator / softmax_total[..., None]).reshape(PIECE_ELEMENTS, HEADS * HD)
    return ((activation_single_precision + skip_coefficient_line * attended).astype(jnp.bfloat16), cached_probe_vectors, cached_payload_vectors)

def reference(perturbed_frame_activation, inbound_activation, section_block_indices, tile_arrival_permutation, adaptive_shifting, adaptive_scaling, tier_query_factor, tier_skip_coefficient, earlier_step_lookup_matrix, earlier_step_content_matrix):
    segment_results = []
    prior_value = None
    for partition_number in range(N_SEGMENT):
        cached_probe_vectors = earlier_step_lookup_matrix[partition_number]
        cached_payload_vectors = earlier_step_content_matrix[partition_number]
        produced_results = []
        for round_counter in range(PATCHES):
            tile_number = tile_arrival_permutation[(round_counter - partition_number) % PATCHES]
            if partition_number == 0:
                passing_vessel = perturbed_frame_activation[tile_arrival_permutation[round_counter]]
            elif round_counter == 0:
                passing_vessel = inbound_activation[partition_number]
            else:
                passing_vessel = prior_value[round_counter - 1]
            for tier_number in range(LMAX):
                live_flag = section_block_indices[partition_number] > tier_number
                latest_activation, latest_probe_vectors, latest_payload_vectors = transform_level(passing_vessel, adaptive_shifting[partition_number, tier_number], adaptive_scaling[partition_number, tier_number], tier_query_factor[partition_number, tier_number], tier_skip_coefficient[partition_number, tier_number], cached_probe_vectors[tier_number], cached_payload_vectors[tier_number], tile_number)
                passing_vessel = jnp.where(live_flag, latest_activation, passing_vessel)
                cached_probe_vectors = cached_probe_vectors.at[tier_number].set(jnp.where(live_flag, latest_probe_vectors, cached_probe_vectors[tier_number]))
                cached_payload_vectors = cached_payload_vectors.at[tier_number].set(jnp.where(live_flag, latest_payload_vectors, cached_payload_vectors[tier_number]))
            produced_results.append(passing_vessel)
        prior_value = produced_results
        segment_results.append(jnp.stack(produced_results))
    return jnp.stack(segment_results)
```

```python
import math

import jax
import jax.numpy as jnp
from jax import lax
from jax.sharding import Mesh
from jax.sharding import PartitionSpec as P

HD = 128
EPSILON = 1e-06

HEAD_AXIS = "cx"
TOKEN_AXES = ("cz", "cc")
CTX_AXES = ("cx", "cz", "cc")


def head_norm(values):
    return values * lax.rsqrt(jnp.mean(values * values, axis=-1, keepdims=True) + EPSILON)


def to_head_groups(rows, groups):
    *lead, n, width = rows.shape
    split = rows.reshape(*lead, n, groups, width // groups)
    return jnp.moveaxis(split, -2, 0)


def per_device(
    perturbed_frame_activation,
    inbound_activation,
    section_block_indices,
    tile_arrival_permutation,
    adaptive_shifting,
    adaptive_scaling,
    tier_query_factor,
    tier_skip_coefficient,
    earlier_step_lookup_matrix,
    earlier_step_content_matrix,
):
    segment = lax.axis_index("segment")
    patch_count = tile_arrival_permutation.shape[0]
    rows = inbound_activation.shape[1]
    width = inbound_activation.shape[2]
    heads = width // HD
    groups = lax.axis_size(HEAD_AXIS)
    group_width = width // groups
    group_heads = heads // groups
    slot_count = earlier_step_lookup_matrix.shape[1]
    layers_here = section_block_indices[0]
    scale = 1.0 / math.sqrt(HD)

    def gather_head_group(kv_rows):
        parts = to_head_groups(kv_rows, groups)
        mine = lax.all_to_all(parts, HEAD_AXIS, 0, 0)
        mine = jnp.moveaxis(mine, 0, -3)
        mine = mine.reshape(*mine.shape[:-3], groups * rows, group_width)
        return lax.all_gather(mine, TOKEN_AXES, axis=mine.ndim - 2, tiled=True)

    other_patch = tile_arrival_permutation[jnp.mod(1 - segment, patch_count)]
    other_k = lax.dynamic_index_in_dim(earlier_step_lookup_matrix[0], other_patch, 1, keepdims=False)
    other_v = lax.dynamic_index_in_dim(earlier_step_content_matrix[0], other_patch, 1, keepdims=False)
    other_kv = gather_head_group(jnp.stack([other_k, other_v], axis=1))

    def layer(state, tier, far_kv):
        live = layers_here > tier
        x = state.astype(jnp.float32)
        hidden = (
            x * lax.rsqrt(jnp.mean(x * x, axis=-1, keepdims=True) + EPSILON)
            * (1.0 + adaptive_scaling[0, tier])
            + adaptive_shifting[0, tier]
        )
        query = head_norm(hidden.reshape(rows, heads, HD)).reshape(rows, width).astype(jnp.bfloat16)
        fresh_key = (
            head_norm((hidden * tier_query_factor[0, tier]).reshape(rows, heads, HD))
            .reshape(rows, width)
            .astype(jnp.bfloat16)
        )
        fresh_value = hidden.astype(jnp.bfloat16)
        packed = to_head_groups(jnp.stack([query, fresh_key, fresh_value]), groups)
        mine = lax.all_to_all(packed, HEAD_AXIS, 0, 0)
        local_q = mine[:, 0].reshape(groups * rows, group_heads, HD)
        near_kv = jnp.moveaxis(mine[:, 1:], 0, 1).reshape(2, groups * rows, group_width)
        near_kv = lax.all_gather(near_kv, TOKEN_AXES, axis=1, tiled=True)
        keys = jnp.concatenate([near_kv[0], far_kv[0]], axis=0)
        values = jnp.concatenate([near_kv[1], far_kv[1]], axis=0)
        key_count = keys.shape[0]
        scores = jnp.einsum(
            "phd,nhd->phn",
            local_q,
            keys.reshape(key_count, group_heads, HD),
            preferred_element_type=jnp.float32,
        ) * scale
        weights = jnp.exp(scores)
        total = jnp.sum(weights, axis=-1)
        numerator = jnp.einsum(
            "phn,nhd->phd",
            weights.astype(jnp.bfloat16),
            values.reshape(key_count, group_heads, HD),
            preferred_element_type=jnp.float32,
        )
        attended = (numerator / total[..., None]).reshape(groups, rows, group_width)
        back = lax.all_to_all(attended, HEAD_AXIS, 0, 0)
        back = jnp.moveaxis(back, 0, 1).reshape(rows, width)
        new_state = (x + tier_skip_coefficient[0, tier] * back).astype(jnp.bfloat16)
        return jnp.where(live, new_state, state), near_kv

    outcomes = []
    state = jnp.where(
        segment == 0,
        lax.dynamic_index_in_dim(perturbed_frame_activation, tile_arrival_permutation[0], 0, keepdims=False),
        inbound_activation[0],
    )
    first_turn_kv = []
    for tier in range(slot_count):
        state, near_kv = layer(state, tier, other_kv[tier])
        first_turn_kv.append(near_kv)
    outcomes.append(state)
    for turn in range(1, patch_count):
        count = lax.axis_size("segment")
        arrived = lax.ppermute(state, "segment", [(i, i + 1) for i in range(count - 1)])
        state = jnp.where(
            segment == 0,
            lax.dynamic_index_in_dim(
                perturbed_frame_activation, tile_arrival_permutation[turn], 0, keepdims=False
            ),
            arrived,
        )
        for tier in range(slot_count):
            state, _ = layer(state, tier, first_turn_kv[tier])
        outcomes.append(state)
    return jnp.stack(outcomes)[None]


def solution(mesh):
    segments, ctx = mesh.devices.shape
    heads_mesh = Mesh(mesh.devices.reshape(segments, 4, ctx // 8, 2), ("segment",) + CTX_AXES)
    return jax.shard_map(
        per_device,
        mesh=heads_mesh,
        in_specs=(
            P(None, CTX_AXES, None),
            P("segment", CTX_AXES, None),
            P("segment"),
            P(),
            P("segment", None, None),
            P("segment", None, None),
            P("segment", None, None),
            P("segment", None, None),
            P("segment", None, None, CTX_AXES, None),
            P("segment", None, None, CTX_AXES, None),
        ),
        out_specs=P("segment", None, CTX_AXES, None),
        check_vma=False,
    )
```

```python
import math

import jax
import jax.numpy as jnp
from jax import lax
from jax.sharding import PartitionSpec as P

HD = 128
EPSILON = 1e-06


def head_norm(values):
    return values * lax.rsqrt(jnp.mean(values * values, axis=-1, keepdims=True) + EPSILON)


def per_device(
    perturbed_frame_activation,
    inbound_activation,
    section_block_indices,
    tile_arrival_permutation,
    adaptive_shifting,
    adaptive_scaling,
    tier_query_factor,
    tier_skip_coefficient,
    earlier_step_lookup_matrix,
    earlier_step_content_matrix,
):
    segment = lax.axis_index("segment")
    place = lax.axis_index("ctx")
    patch_count = tile_arrival_permutation.shape[0]
    rows = inbound_activation.shape[1]
    width = inbound_activation.shape[2]
    heads = width // HD
    slot_count = earlier_step_lookup_matrix.shape[1]
    layers_here = section_block_indices[0]
    scale = 1.0 / math.sqrt(HD)

    def pick_patch(stack, patch, axis):
        return lax.dynamic_index_in_dim(stack, patch, axis, keepdims=False)

    first_rows = jnp.where(
        segment == 0,
        pick_patch(perturbed_frame_activation, tile_arrival_permutation[0], 0),
        inbound_activation[0],
    )
    entry_rows = [first_rows[None]]
    for turn in range(1, patch_count):
        entry_rows.append(pick_patch(perturbed_frame_activation, tile_arrival_permutation[turn], 0)[None])
    other_patch = tile_arrival_permutation[jnp.mod(1 - segment, patch_count)]
    far_k = pick_patch(earlier_step_lookup_matrix[0], other_patch, 1)
    far_v = pick_patch(earlier_step_content_matrix[0], other_patch, 1)
    packed = jnp.concatenate(entry_rows + [far_k, far_v], axis=0)
    whole = lax.all_gather(packed, "ctx", axis=1, tiled=True)
    entry = whole[:patch_count]
    far_k = whole[patch_count : patch_count + slot_count]
    far_v = whole[patch_count + slot_count :]
    tokens = whole.shape[1]

    def layer(state, tier, keys_far, values_far):
        live = layers_here > tier
        x = state.astype(jnp.float32)
        hidden = (
            x * lax.rsqrt(jnp.mean(x * x, axis=-1, keepdims=True) + EPSILON)
            * (1.0 + adaptive_scaling[0, tier])
            + adaptive_shifting[0, tier]
        )
        query = head_norm(hidden.reshape(tokens, heads, HD)).astype(jnp.bfloat16)
        fresh_key = head_norm((hidden * tier_query_factor[0, tier]).reshape(tokens, heads, HD)).astype(
            jnp.bfloat16
        )
        fresh_value = hidden.astype(jnp.bfloat16).reshape(tokens, heads, HD)
        keys = jnp.concatenate([fresh_key, keys_far.reshape(tokens, heads, HD)], axis=0)
        values = jnp.concatenate([fresh_value, values_far.reshape(tokens, heads, HD)], axis=0)
        scores = jnp.einsum("phd,nhd->phn", query, keys, preferred_element_type=jnp.float32) * scale
        weights = jnp.exp(scores)
        total = jnp.sum(weights, axis=-1)
        numerator = jnp.einsum(
            "phn,nhd->phd", weights.astype(jnp.bfloat16), values, preferred_element_type=jnp.float32
        )
        attended = (numerator / total[..., None]).reshape(tokens, width)
        new_state = (x + tier_skip_coefficient[0, tier] * attended).astype(jnp.bfloat16)
        return jnp.where(live, new_state, state), fresh_key.reshape(tokens, width), fresh_value.reshape(
            tokens, width
        )

    def own_rows(state):
        return lax.dynamic_slice_in_dim(state, place * rows, rows, 0)

    outcomes = []
    state = entry[0]
    turn_zero_kv = []
    for tier in range(slot_count):
        state, fresh_key, fresh_value = layer(state, tier, far_k[tier], far_v[tier])
        turn_zero_kv.append((fresh_key, fresh_value))
    outcomes.append(own_rows(state))
    count = lax.axis_size("segment")
    for turn in range(1, patch_count):
        arrived = lax.ppermute(state, "segment", [(i, i + 1) for i in range(count - 1)])
        state = jnp.where(segment == 0, entry[turn], arrived)
        for tier in range(slot_count):
            state, _, _ = layer(state, tier, *turn_zero_kv[tier])
        outcomes.append(own_rows(state))
    return jnp.stack(outcomes)[None]


def solution(mesh):
    return jax.shard_map(
        per_device,
        mesh=mesh,
        in_specs=(
            P(None, "ctx", None),
            P("segment", "ctx", None),
            P("segment"),
            P(),
            P("segment", None, None),
            P("segment", None, None),
            P("segment", None, None),
            P("segment", None, None),
            P("segment", None, None, "ctx", None),
            P("segment", None, None, "ctx", None),
        ),
        out_specs=P("segment", None, "ctx", None),
        check_vma=False,
    )
```

```python
import math

import jax
import jax.numpy as jnp
from jax import lax
from jax.experimental import pallas as pl
from jax.sharding import PartitionSpec as P

HD = 128
EPSILON = 1e-06


def head_norm(values):
    return values * lax.rsqrt(jnp.mean(values * values, axis=-1, keepdims=True) + EPSILON)


def attention_kernel(q_ref, kn_ref, kf_ref, vn_ref, vf_ref, x_ref, skip_ref, o_ref):
    scale = 1.0 / math.sqrt(HD)
    dims = (((1,), (1,)), ((), ()))
    for j in range(q_ref.shape[1] // HD):
        cols = slice(j * HD, (j + 1) * HD)
        query = q_ref[:, cols]
        near = lax.dot_general(query, kn_ref[:, cols], dims, preferred_element_type=jnp.float32) * scale
        far = lax.dot_general(query, kf_ref[:, cols], dims, preferred_element_type=jnp.float32) * scale
        near = jnp.exp(near)
        far = jnp.exp(far)
        total = jnp.sum(near, axis=-1, keepdims=True) + jnp.sum(far, axis=-1, keepdims=True)
        numerator = jnp.dot(
            near.astype(jnp.bfloat16), vn_ref[:, cols], preferred_element_type=jnp.float32
        ) + jnp.dot(far.astype(jnp.bfloat16), vf_ref[:, cols], preferred_element_type=jnp.float32)
        attended = numerator / total
        x = x_ref[:, cols].astype(jnp.float32)
        o_ref[:, cols] = (x + skip_ref[:, cols] * attended).astype(o_ref.dtype)


def attend_and_add(query, near_k, far_k, near_v, far_v, state, skip, block=384):
    tokens, width = state.shape
    tile = pl.BlockSpec((tokens, block), lambda i: (0, i))
    return pl.pallas_call(
        attention_kernel,
        out_shape=jax.ShapeDtypeStruct((tokens, width), jnp.bfloat16),
        grid=(width // block,),
        in_specs=[tile] * 6 + [pl.BlockSpec((1, block), lambda i: (0, i))],
        out_specs=tile,
        cost_estimate=pl.CostEstimate(
            flops=8 * tokens * 2 * tokens * width,
            transcendentals=tokens * 2 * tokens * (width // HD),
            bytes_accessed=7 * tokens * width * 2,
        ),
    )(query, near_k, far_k, near_v, far_v, state, skip.reshape(1, width))


def per_device(
    perturbed_frame_activation,
    inbound_activation,
    section_block_indices,
    tile_arrival_permutation,
    adaptive_shifting,
    adaptive_scaling,
    tier_query_factor,
    tier_skip_coefficient,
    earlier_step_lookup_matrix,
    earlier_step_content_matrix,
):
    segment = lax.axis_index("segment")
    place = lax.axis_index("ctx")
    patch_count = tile_arrival_permutation.shape[0]
    rows = inbound_activation.shape[1]
    width = inbound_activation.shape[2]
    heads = width // HD
    slot_count = earlier_step_lookup_matrix.shape[1]
    layers_here = section_block_indices[0]

    def pick_patch(stack, patch, axis):
        return lax.dynamic_index_in_dim(stack, patch, axis, keepdims=False)

    first_rows = jnp.where(
        segment == 0,
        pick_patch(perturbed_frame_activation, tile_arrival_permutation[0], 0),
        inbound_activation[0],
    )
    entry_rows = [first_rows[None]]
    for turn in range(1, patch_count):
        entry_rows.append(pick_patch(perturbed_frame_activation, tile_arrival_permutation[turn], 0)[None])
    other_patch = tile_arrival_permutation[jnp.mod(1 - segment, patch_count)]
    far_k = pick_patch(earlier_step_lookup_matrix[0], other_patch, 1)
    far_v = pick_patch(earlier_step_content_matrix[0], other_patch, 1)
    packed = jnp.concatenate(entry_rows + [far_k, far_v], axis=0)
    whole = lax.all_gather(packed, "ctx", axis=1, tiled=True)
    entry = whole[:patch_count]
    far_k = whole[patch_count : patch_count + slot_count]
    far_v = whole[patch_count + slot_count :]
    tokens = whole.shape[1]

    def layer(state, tier, keys_far, values_far):
        live = layers_here > tier
        x = state.astype(jnp.float32)
        hidden = (
            x * lax.rsqrt(jnp.mean(x * x, axis=-1, keepdims=True) + EPSILON)
            * (1.0 + adaptive_scaling[0, tier])
            + adaptive_shifting[0, tier]
        )
        query = head_norm(hidden.reshape(tokens, heads, HD)).reshape(tokens, width).astype(jnp.bfloat16)
        fresh_key = (
            head_norm((hidden * tier_query_factor[0, tier]).reshape(tokens, heads, HD))
            .reshape(tokens, width)
            .astype(jnp.bfloat16)
        )
        fresh_value = hidden.astype(jnp.bfloat16)
        new_state = attend_and_add(
            query, fresh_key, keys_far, fresh_value, values_far, state, tier_skip_coefficient[0, tier]
        )
        return jnp.where(live, new_state, state), fresh_key, fresh_value

    def own_rows(state):
        return lax.dynamic_slice_in_dim(state, place * rows, rows, 0)

    outcomes = []
    state = entry[0]
    turn_zero_kv = []
    for tier in range(slot_count):
        state, fresh_key, fresh_value = layer(state, tier, far_k[tier], far_v[tier])
        turn_zero_kv.append((fresh_key, fresh_value))
    outcomes.append(own_rows(state))
    count = lax.axis_size("segment")
    for turn in range(1, patch_count):
        arrived = lax.ppermute(state, "segment", [(i, i + 1) for i in range(count - 1)])
        state = jnp.where(segment == 0, entry[turn], arrived)
        for tier in range(slot_count):
            state, _, _ = layer(state, tier, *turn_zero_kv[tier])
        outcomes.append(own_rows(state))
    return jnp.stack(outcomes)[None]


def solution(mesh):
    return jax.shard_map(
        per_device,
        mesh=mesh,
        in_specs=(
            P(None, "ctx", None),
            P("segment", "ctx", None),
            P("segment"),
            P(),
            P("segment", None, None),
            P("segment", None, None),
            P("segment", None, None),
            P("segment", None, None),
            P("segment", None, None, "ctx", None),
            P("segment", None, None, "ctx", None),
        ),
        out_specs=P("segment", None, "ctx", None),
        check_vma=False,
    )
```

```python
import math

import jax
import jax.numpy as jnp
from jax import lax
from jax.experimental import pallas as pl
from jax.sharding import PartitionSpec as P

HD = 128
EPSILON = 1e-06


def head_norm(values):
    return values * lax.rsqrt(jnp.mean(values * values, axis=-1, keepdims=True) + EPSILON)


def layer_kernel(
    full_ref, x_ref, shift_ref, stretch_ref, factor_ref, skip_ref, kf_ref, vf_ref, o_ref, k_ref, v_ref
):
    scale = 1.0 / math.sqrt(HD)
    dims = (((1,), (1,)), ((), ()))
    whole = full_ref[...].astype(jnp.float32)
    row_scale = lax.rsqrt(jnp.mean(whole * whole, axis=-1, keepdims=True) + EPSILON)
    for j in range(x_ref.shape[1] // HD):
        cols = slice(j * HD, (j + 1) * HD)
        x = x_ref[:, cols].astype(jnp.float32)
        hidden = x * row_scale * (1.0 + stretch_ref[:, cols]) + shift_ref[:, cols]
        query = head_norm(hidden).astype(jnp.bfloat16)
        fresh_key = head_norm(hidden * factor_ref[:, cols]).astype(jnp.bfloat16)
        fresh_value = hidden.astype(jnp.bfloat16)
        k_ref[:, cols] = fresh_key
        v_ref[:, cols] = fresh_value
        near = lax.dot_general(query, fresh_key, dims, preferred_element_type=jnp.float32) * scale
        far = lax.dot_general(query, kf_ref[:, cols], dims, preferred_element_type=jnp.float32) * scale
        near = jnp.exp(near)
        far = jnp.exp(far)
        total = jnp.sum(near, axis=-1, keepdims=True) + jnp.sum(far, axis=-1, keepdims=True)
        numerator = jnp.dot(
            near.astype(jnp.bfloat16), fresh_value, preferred_element_type=jnp.float32
        ) + jnp.dot(far.astype(jnp.bfloat16), vf_ref[:, cols], preferred_element_type=jnp.float32)
        attended = numerator / total
        o_ref[:, cols] = (x + skip_ref[:, cols] * attended).astype(o_ref.dtype)


def fused_layer(state, shift, stretch, factor, skip, far_k, far_v, block=384):
    tokens, width = state.shape
    tile = pl.BlockSpec((tokens, block), lambda i: (0, i))
    line = pl.BlockSpec((1, block), lambda i: (0, i))
    out = jax.ShapeDtypeStruct((tokens, width), jnp.bfloat16)
    return pl.pallas_call(
        layer_kernel,
        out_shape=(out, out, out),
        grid=(width // block,),
        in_specs=[pl.BlockSpec((tokens, width), lambda i: (0, 0)), tile, line, line, line, line, tile, tile],
        out_specs=(tile, tile, tile),
        cost_estimate=pl.CostEstimate(
            flops=8 * tokens * 2 * tokens * width,
            transcendentals=tokens * 2 * tokens * (width // HD),
            bytes_accessed=7 * tokens * width * 2,
        ),
    )(
        state,
        state,
        shift.reshape(1, width),
        stretch.reshape(1, width),
        factor.reshape(1, width),
        skip.reshape(1, width),
        far_k,
        far_v,
    )


def per_device(
    perturbed_frame_activation,
    inbound_activation,
    section_block_indices,
    tile_arrival_permutation,
    adaptive_shifting,
    adaptive_scaling,
    tier_query_factor,
    tier_skip_coefficient,
    earlier_step_lookup_matrix,
    earlier_step_content_matrix,
):
    segment = lax.axis_index("segment")
    place = lax.axis_index("ctx")
    patch_count = tile_arrival_permutation.shape[0]
    rows = inbound_activation.shape[1]
    width = inbound_activation.shape[2]
    slot_count = earlier_step_lookup_matrix.shape[1]
    layers_here = section_block_indices[0]

    def pick_patch(stack, patch, axis):
        return lax.dynamic_index_in_dim(stack, patch, axis, keepdims=False)

    first_rows = jnp.where(
        segment == 0,
        pick_patch(perturbed_frame_activation, tile_arrival_permutation[0], 0),
        inbound_activation[0],
    )
    entry_rows = [first_rows[None]]
    for turn in range(1, patch_count):
        entry_rows.append(pick_patch(perturbed_frame_activation, tile_arrival_permutation[turn], 0)[None])
    other_patch = tile_arrival_permutation[jnp.mod(1 - segment, patch_count)]
    far_k = pick_patch(earlier_step_lookup_matrix[0], other_patch, 1)
    far_v = pick_patch(earlier_step_content_matrix[0], other_patch, 1)
    packed = jnp.concatenate(entry_rows + [far_k, far_v], axis=0)
    whole = lax.all_gather(packed, "ctx", axis=1, tiled=True)
    entry = whole[:patch_count]
    far_k = whole[patch_count : patch_count + slot_count]
    far_v = whole[patch_count + slot_count :]
    tokens = whole.shape[1]

    def layer(state, tier, keys_far, values_far):
        live = layers_here > tier
        new_state, fresh_key, fresh_value = fused_layer(
            state,
            adaptive_shifting[0, tier],
            adaptive_scaling[0, tier],
            tier_query_factor[0, tier],
            tier_skip_coefficient[0, tier],
            keys_far,
            values_far,
        )
        return jnp.where(live, new_state, state), fresh_key, fresh_value

    def own_rows(state):
        return lax.dynamic_slice_in_dim(state, place * rows, rows, 0)

    outcomes = []
    state = entry[0]
    turn_zero_kv = []
    for tier in range(slot_count):
        state, fresh_key, fresh_value = layer(state, tier, far_k[tier], far_v[tier])
        turn_zero_kv.append((fresh_key, fresh_value))
    outcomes.append(own_rows(state))
    count = lax.axis_size("segment")
    for turn in range(1, patch_count):
        arrived = lax.ppermute(state, "segment", [(i, i + 1) for i in range(count - 1)])
        state = jnp.where(segment == 0, entry[turn], arrived)
        for tier in range(slot_count):
            state, _, _ = layer(state, tier, *turn_zero_kv[tier])
        outcomes.append(own_rows(state))
    return jnp.stack(outcomes)[None]


def solution(mesh):
    return jax.shard_map(
        per_device,
        mesh=mesh,
        in_specs=(
            P(None, "ctx", None),
            P("segment", "ctx", None),
            P("segment"),
            P(),
            P("segment", None, None),
            P("segment", None, None),
            P("segment", None, None),
            P("segment", None, None),
            P("segment", None, None, "ctx", None),
            P("segment", None, None, "ctx", None),
        ),
        out_specs=P("segment", None, "ctx", None),
        check_vma=False,
    )
```

```python
import functools
import math

import jax
import jax.numpy as jnp
from jax import lax
from jax.experimental import pallas as pl
from jax.experimental.pallas import tpu as pltpu
from jax.sharding import PartitionSpec as P

HD = 128
EPSILON = 1e-06


def head_norm(values):
    return values * lax.rsqrt(jnp.mean(values * values, axis=-1, keepdims=True) + EPSILON)


def layer_kernel(flags_ref, *refs, two_sources, keep_kv):
    if two_sources:
        full_ref, x_ref, entry_full_ref, entry_x_ref, *refs = refs
    else:
        full_ref, x_ref, *refs = refs
    shift_ref, stretch_ref, factor_ref, skip_ref, kf_ref, vf_ref, o_ref, *kv_refs = refs
    live = flags_ref[0] > 0
    scale = 1.0 / math.sqrt(HD)
    dims = (((1,), (1,)), ((), ()))
    whole = full_ref[...]
    state = x_ref[...]
    if two_sources:
        use_entry = flags_ref[1] > 0
        whole = jnp.where(use_entry, entry_full_ref[...], whole)
        state = jnp.where(use_entry, entry_x_ref[...], state)
    whole = whole.astype(jnp.float32)
    row_scale = lax.rsqrt(jnp.mean(whole * whole, axis=-1, keepdims=True) + EPSILON)
    for j in range(state.shape[1] // HD):
        cols = slice(j * HD, (j + 1) * HD)
        x_rounded = state[:, cols]
        x = x_rounded.astype(jnp.float32)
        hidden = x * row_scale * (1.0 + stretch_ref[:, cols]) + shift_ref[:, cols]
        query = head_norm(hidden).astype(jnp.bfloat16)
        fresh_key = head_norm(hidden * factor_ref[:, cols]).astype(jnp.bfloat16)
        fresh_value = hidden.astype(jnp.bfloat16)
        if keep_kv:
            kv_refs[0][:, cols] = fresh_key
            kv_refs[1][:, cols] = fresh_value
        near = lax.dot_general(query, fresh_key, dims, preferred_element_type=jnp.float32) * scale
        far = lax.dot_general(query, kf_ref[:, cols], dims, preferred_element_type=jnp.float32) * scale
        near = jnp.exp(near)
        far = jnp.exp(far)
        total = jnp.sum(near, axis=-1, keepdims=True) + jnp.sum(far, axis=-1, keepdims=True)
        numerator = jnp.dot(
            near.astype(jnp.bfloat16), fresh_value, preferred_element_type=jnp.float32
        ) + jnp.dot(far.astype(jnp.bfloat16), vf_ref[:, cols], preferred_element_type=jnp.float32)
        attended = numerator / total
        new_state = (x + skip_ref[:, cols] * attended).astype(o_ref.dtype)
        o_ref[:, cols] = jnp.where(live, new_state, x_rounded)


def fused_layer(flags, source, params, tier, far_k, far_v, entry=None, keep_kv=True, block=384):
    array, slab = source
    _, tokens, width = array.shape

    def slab_specs(slab_index):
        return [
            pl.BlockSpec((None, tokens, width), lambda i, f: (slab_index, 0, 0)),
            pl.BlockSpec((None, tokens, block), lambda i, f: (slab_index, 0, i)),
        ]

    def tile_of(slab_index):
        return pl.BlockSpec((None, tokens, block), lambda i, f: (slab_index, 0, i))

    line = pl.BlockSpec((None, 1, block), lambda i, f: (tier, 0, i))
    in_specs = slab_specs(slab)
    operands = [array, array]
    if entry is not None:
        in_specs += slab_specs(entry[1])
        operands += [entry[0], entry[0]]
    in_specs += [line] * 4 + [tile_of(far_k[1]), tile_of(far_v[1])]
    operands += [p.reshape(p.shape[0], 1, width) for p in params] + [far_k[0], far_v[0]]
    out_tile = pl.BlockSpec((tokens, block), lambda i, f: (0, i))
    out = jax.ShapeDtypeStruct((tokens, width), jnp.bfloat16)
    count = 3 if keep_kv else 1
    results = pl.pallas_call(
        functools.partial(layer_kernel, two_sources=entry is not None, keep_kv=keep_kv),
        out_shape=(out,) * count,
        grid_spec=pltpu.PrefetchScalarGridSpec(
            num_scalar_prefetch=1,
            grid=(width // block,),
            in_specs=in_specs,
            out_specs=(out_tile,) * count,
        ),
        cost_estimate=pl.CostEstimate(
            flops=8 * tokens * 2 * tokens * width,
            transcendentals=tokens * 2 * tokens * (width // HD),
            bytes_accessed=(4 + 2 * count) * tokens * width,
        ),
    )(flags, *operands)
    return results if keep_kv else (results[0], None, None)


def per_device(
    perturbed_frame_activation,
    inbound_activation,
    section_block_indices,
    tile_arrival_permutation,
    adaptive_shifting,
    adaptive_scaling,
    tier_query_factor,
    tier_skip_coefficient,
    earlier_step_lookup_matrix,
    earlier_step_content_matrix,
):
    segment = lax.axis_index("segment")
    place = lax.axis_index("ctx")
    patch_count = tile_arrival_permutation.shape[0]
    rows = inbound_activation.shape[1]
    width = inbound_activation.shape[2]
    slot_count = earlier_step_lookup_matrix.shape[1]
    layers_here = section_block_indices[0]

    def pick_patch(stack, patch, axis):
        return lax.dynamic_index_in_dim(stack, patch, axis, keepdims=False)

    first_rows = jnp.where(
        segment == 0,
        pick_patch(perturbed_frame_activation, tile_arrival_permutation[0], 0),
        inbound_activation[0],
    )
    entry_rows = [first_rows[None]]
    for turn in range(1, patch_count):
        entry_rows.append(pick_patch(perturbed_frame_activation, tile_arrival_permutation[turn], 0)[None])
    other_patch = tile_arrival_permutation[jnp.mod(1 - segment, patch_count)]
    far_k = pick_patch(earlier_step_lookup_matrix[0], other_patch, 1)
    far_v = pick_patch(earlier_step_content_matrix[0], other_patch, 1)
    packed = jnp.concatenate(entry_rows + [far_k, far_v], axis=0)
    whole = lax.all_gather(packed, "ctx", axis=1, tiled=True)
    params = [
        adaptive_shifting[0],
        adaptive_scaling[0],
        tier_query_factor[0],
        tier_skip_coefficient[0],
    ]
    first_segment = (segment == 0).astype(jnp.int32)

    def flags(tier):
        return jnp.stack([(layers_here > tier).astype(jnp.int32), first_segment])

    def own_rows(state):
        return lax.dynamic_slice_in_dim(state, place * rows, rows, 0)

    outcomes = []
    source = (whole, 0)
    turn_zero_kv = []
    for tier in range(slot_count):
        state, fresh_key, fresh_value = fused_layer(
            flags(tier),
            source,
            params,
            tier,
            (whole, patch_count + tier),
            (whole, patch_count + slot_count + tier),
        )
        source = (state[None], 0)
        turn_zero_kv.append(((fresh_key[None], 0), (fresh_value[None], 0)))
    outcomes.append(own_rows(state))
    count = lax.axis_size("segment")
    for turn in range(1, patch_count):
        arrived = lax.ppermute(state, "segment", [(i, i + 1) for i in range(count - 1)])
        source = (arrived[None], 0)
        entry = (whole, turn)
        for tier in range(slot_count):
            state, _, _ = fused_layer(
                flags(tier), source, params, tier, *turn_zero_kv[tier], entry=entry, keep_kv=False
            )
            source = (state[None], 0)
            entry = None
        outcomes.append(own_rows(state))
    return jnp.stack(outcomes)[None]


def solution(mesh):
    return jax.shard_map(
        per_device,
        mesh=mesh,
        in_specs=(
            P(None, "ctx", None),
            P("segment", "ctx", None),
            P("segment"),
            P(),
            P("segment", None, None),
            P("segment", None, None),
            P("segment", None, None),
            P("segment", None, None),
            P("segment", None, None, "ctx", None),
            P("segment", None, None, "ctx", None),
        ),
        out_specs=P("segment", None, "ctx", None),
        check_vma=False,
    )
```

```python
import functools
import math

import jax
import jax.numpy as jnp
from jax import lax
from jax.experimental import pallas as pl
from jax.experimental.pallas import tpu as pltpu
from jax.sharding import PartitionSpec as P

HD = 128
EPSILON = 1e-06


def head_norm(values):
    return values * lax.rsqrt(jnp.mean(values * values, axis=-1, keepdims=True) + EPSILON)


def layer_kernel(flags_ref, *refs, two_sources, keep_kv):
    if two_sources:
        full_ref, x_ref, entry_full_ref, entry_x_ref, *refs = refs
    else:
        full_ref, x_ref, *refs = refs
    shift_ref, stretch_ref, factor_ref, skip_ref, kf_ref, vf_ref, o_ref, *kv_refs = refs
    live = flags_ref[0] > 0
    scale = 1.0 / math.sqrt(HD)
    dims = (((1,), (1,)), ((), ()))
    whole = full_ref[...]
    state = x_ref[...]
    if two_sources:
        use_entry = flags_ref[1] > 0
        whole = jnp.where(use_entry, entry_full_ref[...], whole)
        state = jnp.where(use_entry, entry_x_ref[...], state)
    whole = whole.astype(jnp.float32)
    row_scale = lax.rsqrt(jnp.mean(whole * whole, axis=-1, keepdims=True) + EPSILON)
    for j in range(state.shape[1] // HD):
        cols = slice(j * HD, (j + 1) * HD)
        x_rounded = state[:, cols]
        x = x_rounded.astype(jnp.float32)
        hidden = x * row_scale * (1.0 + stretch_ref[:, cols]) + shift_ref[:, cols]
        query = head_norm(hidden).astype(jnp.bfloat16)
        fresh_key = head_norm(hidden * factor_ref[:, cols]).astype(jnp.bfloat16)
        fresh_value = hidden.astype(jnp.bfloat16)
        if keep_kv:
            kv_refs[0][:, cols] = fresh_key
            kv_refs[1][:, cols] = fresh_value
        near = lax.dot_general(query, fresh_key, dims, preferred_element_type=jnp.float32) * scale
        far = lax.dot_general(query, kf_ref[:, cols], dims, preferred_element_type=jnp.float32) * scale
        near = jnp.exp(near)
        far = jnp.exp(far)
        total = jnp.sum(near, axis=-1, keepdims=True) + jnp.sum(far, axis=-1, keepdims=True)
        numerator = jnp.dot(
            near.astype(jnp.bfloat16), fresh_value, preferred_element_type=jnp.float32
        ) + jnp.dot(far.astype(jnp.bfloat16), vf_ref[:, cols], preferred_element_type=jnp.float32)
        attended = numerator / total
        new_state = (x + skip_ref[:, cols] * attended).astype(o_ref.dtype)
        o_ref[:, cols] = jnp.where(live, new_state, x_rounded)


def fused_layer(flags, source, params, tier, far_k, far_v, entry=None, keep_kv=True, block=1536):
    array, slab = source
    _, tokens, width = array.shape

    def slab_specs(slab_index):
        return [
            pl.BlockSpec((None, tokens, width), lambda i, f: (slab_index, 0, 0)),
            pl.BlockSpec((None, tokens, block), lambda i, f: (slab_index, 0, i)),
        ]

    def tile_of(slab_index):
        return pl.BlockSpec((None, tokens, block), lambda i, f: (slab_index, 0, i))

    line = pl.BlockSpec((None, 1, block), lambda i, f: (tier, 0, i))
    in_specs = slab_specs(slab)
    operands = [array, array]
    if entry is not None:
        in_specs += slab_specs(entry[1])
        operands += [entry[0], entry[0]]
    in_specs += [line] * 4 + [tile_of(far_k[1]), tile_of(far_v[1])]
    operands += [p.reshape(p.shape[0], 1, width) for p in params] + [far_k[0], far_v[0]]
    out_tile = pl.BlockSpec((tokens, block), lambda i, f: (0, i))
    out = jax.ShapeDtypeStruct((tokens, width), jnp.bfloat16)
    count = 3 if keep_kv else 1
    results = pl.pallas_call(
        functools.partial(layer_kernel, two_sources=entry is not None, keep_kv=keep_kv),
        out_shape=(out,) * count,
        grid_spec=pltpu.PrefetchScalarGridSpec(
            num_scalar_prefetch=1,
            grid=(width // block,),
            in_specs=in_specs,
            out_specs=(out_tile,) * count,
        ),
        cost_estimate=pl.CostEstimate(
            flops=8 * tokens * 2 * tokens * width,
            transcendentals=tokens * 2 * tokens * (width // HD),
            bytes_accessed=(4 + 2 * count) * tokens * width,
        ),
    )(flags, *operands)
    return results if keep_kv else (results[0], None, None)


def per_device(
    perturbed_frame_activation,
    inbound_activation,
    section_block_indices,
    tile_arrival_permutation,
    adaptive_shifting,
    adaptive_scaling,
    tier_query_factor,
    tier_skip_coefficient,
    earlier_step_lookup_matrix,
    earlier_step_content_matrix,
):
    segment = lax.axis_index("segment")
    place = lax.axis_index("ctx")
    patch_count = tile_arrival_permutation.shape[0]
    rows = inbound_activation.shape[1]
    width = inbound_activation.shape[2]
    slot_count = earlier_step_lookup_matrix.shape[1]
    layers_here = section_block_indices[0]

    def pick_patch(stack, patch, axis):
        return lax.dynamic_index_in_dim(stack, patch, axis, keepdims=False)

    first_rows = jnp.where(
        segment == 0,
        pick_patch(perturbed_frame_activation, tile_arrival_permutation[0], 0),
        inbound_activation[0],
    )
    entry_rows = [first_rows[None]]
    for turn in range(1, patch_count):
        entry_rows.append(pick_patch(perturbed_frame_activation, tile_arrival_permutation[turn], 0)[None])
    other_patch = tile_arrival_permutation[jnp.mod(1 - segment, patch_count)]
    far_k = pick_patch(earlier_step_lookup_matrix[0], other_patch, 1)
    far_v = pick_patch(earlier_step_content_matrix[0], other_patch, 1)
    packed = jnp.concatenate(entry_rows + [far_k, far_v], axis=0)
    whole = lax.all_gather(packed, "ctx", axis=1, tiled=True)
    params = [
        adaptive_shifting[0],
        adaptive_scaling[0],
        tier_query_factor[0],
        tier_skip_coefficient[0],
    ]
    first_segment = (segment == 0).astype(jnp.int32)

    def flags(tier):
        return jnp.stack([(layers_here > tier).astype(jnp.int32), first_segment])

    def own_rows(state):
        return lax.dynamic_slice_in_dim(state, place * rows, rows, 0)

    outcomes = []
    source = (whole, 0)
    turn_zero_kv = []
    for tier in range(slot_count):
        state, fresh_key, fresh_value = fused_layer(
            flags(tier),
            source,
            params,
            tier,
            (whole, patch_count + tier),
            (whole, patch_count + slot_count + tier),
        )
        source = (state[None], 0)
        turn_zero_kv.append(((fresh_key[None], 0), (fresh_value[None], 0)))
    outcomes.append(own_rows(state))
    count = lax.axis_size("segment")
    for turn in range(1, patch_count):
        arrived = lax.ppermute(state, "segment", [(i, i + 1) for i in range(count - 1)])
        source = (arrived[None], 0)
        entry = (whole, turn)
        for tier in range(slot_count):
            state, _, _ = fused_layer(
                flags(tier), source, params, tier, *turn_zero_kv[tier], entry=entry, keep_kv=False
            )
            source = (state[None], 0)
            entry = None
        outcomes.append(own_rows(state))
    return jnp.stack(outcomes)[None]


def solution(mesh):
    return jax.shard_map(
        per_device,
        mesh=mesh,
        in_specs=(
            P(None, "ctx", None),
            P("segment", "ctx", None),
            P("segment"),
            P(),
            P("segment", None, None),
            P("segment", None, None),
            P("segment", None, None),
            P("segment", None, None),
            P("segment", None, None, "ctx", None),
            P("segment", None, None, "ctx", None),
        ),
        out_specs=P("segment", None, "ctx", None),
        check_vma=False,
    )
```

```python
import functools
import math

import jax
import jax.numpy as jnp
from jax import lax
from jax.experimental import pallas as pl
from jax.experimental.pallas import tpu as pltpu
from jax.sharding import PartitionSpec as P

HD = 128
EPSILON = 1e-06


def head_norm(values):
    return values * lax.rsqrt(jnp.mean(values * values, axis=-1, keepdims=True) + EPSILON)


def layer_kernel(flags_ref, *refs, two_sources, keep_kv):
    if two_sources:
        full_ref, x_ref, entry_full_ref, entry_x_ref, *refs = refs
    else:
        full_ref, x_ref, *refs = refs
    shift_ref, stretch_ref, factor_ref, skip_ref, kf_ref, vf_ref, o_ref, *kv_refs = refs
    live = flags_ref[0] > 0
    scale = 1.0 / math.sqrt(HD)
    dims = (((1,), (1,)), ((), ()))
    whole = full_ref[...]
    state = x_ref[...]
    if two_sources:
        use_entry = flags_ref[1] > 0
        whole = jnp.where(use_entry, entry_full_ref[...], whole)
        state = jnp.where(use_entry, entry_x_ref[...], state)
    whole = whole.astype(jnp.float32)
    row_scale = lax.rsqrt(jnp.mean(whole * whole, axis=-1, keepdims=True) + EPSILON)
    for j in range(state.shape[1] // HD):
        cols = slice(j * HD, (j + 1) * HD)
        x_rounded = state[:, cols]
        x = x_rounded.astype(jnp.float32)
        hidden = x * row_scale * (1.0 + stretch_ref[:, cols]) + shift_ref[:, cols]
        query = head_norm(hidden).astype(jnp.bfloat16)
        fresh_key = head_norm(hidden * factor_ref[:, cols]).astype(jnp.bfloat16)
        fresh_value = hidden.astype(jnp.bfloat16)
        if keep_kv:
            kv_refs[0][:, cols] = fresh_key
            kv_refs[1][:, cols] = fresh_value
        near = lax.dot_general(query, fresh_key, dims, preferred_element_type=jnp.float32) * scale
        far = lax.dot_general(query, kf_ref[:, cols], dims, preferred_element_type=jnp.float32) * scale
        near = jnp.exp(near)
        far = jnp.exp(far)
        total = jnp.sum(near, axis=-1, keepdims=True) + jnp.sum(far, axis=-1, keepdims=True)
        numerator = jnp.dot(
            near.astype(jnp.bfloat16), fresh_value, preferred_element_type=jnp.float32
        ) + jnp.dot(far.astype(jnp.bfloat16), vf_ref[:, cols], preferred_element_type=jnp.float32)
        attended = numerator / total
        new_state = (x + skip_ref[:, cols] * attended).astype(o_ref.dtype)
        o_ref[:, cols] = jnp.where(live, new_state, x_rounded)


def fused_layer(flags, source, params, tier, far_k, far_v, entry=None, keep_kv=True, block=1536):
    array, slab = source
    _, tokens, width = array.shape

    def slab_specs(slab_index):
        return [
            pl.BlockSpec((None, tokens, width), lambda i, f: (slab_index, 0, 0)),
            pl.BlockSpec((None, tokens, block), lambda i, f: (slab_index, 0, i)),
        ]

    def tile_of(slab_index):
        return pl.BlockSpec((None, tokens, block), lambda i, f: (slab_index, 0, i))

    line = pl.BlockSpec((None, 1, block), lambda i, f: (tier, 0, i))
    in_specs = slab_specs(slab)
    operands = [array, array]
    if entry is not None:
        in_specs += slab_specs(entry[1])
        operands += [entry[0], entry[0]]
    in_specs += [line] * 4 + [tile_of(far_k[1]), tile_of(far_v[1])]
    operands += [p.reshape(p.shape[0], 1, width) for p in params] + [far_k[0], far_v[0]]
    out_tile = pl.BlockSpec((tokens, block), lambda i, f: (0, i))
    out = jax.ShapeDtypeStruct((tokens, width), jnp.bfloat16)
    count = 3 if keep_kv else 1
    results = pl.pallas_call(
        functools.partial(layer_kernel, two_sources=entry is not None, keep_kv=keep_kv),
        out_shape=(out,) * count,
        grid_spec=pltpu.PrefetchScalarGridSpec(
            num_scalar_prefetch=1,
            grid=(width // block,),
            in_specs=in_specs,
            out_specs=(out_tile,) * count,
        ),
        cost_estimate=pl.CostEstimate(
            flops=8 * tokens * 2 * tokens * width,
            transcendentals=tokens * 2 * tokens * (width // HD),
            bytes_accessed=(4 + 2 * count) * tokens * width,
        ),
    )(flags, *operands)
    return results if keep_kv else (results[0], None, None)


def per_device(
    perturbed_frame_activation,
    inbound_activation,
    section_block_indices,
    tile_arrival_permutation,
    adaptive_shifting,
    adaptive_scaling,
    tier_query_factor,
    tier_skip_coefficient,
    earlier_step_lookup_matrix,
    earlier_step_content_matrix,
):
    segment = lax.axis_index("segment")
    place = lax.axis_index("ctx")
    patch_count = tile_arrival_permutation.shape[0]
    rows = inbound_activation.shape[1]
    width = inbound_activation.shape[2]
    slot_count = earlier_step_lookup_matrix.shape[1]
    layers_here = section_block_indices[0]

    def pick_patch(stack, patch, axis):
        return lax.dynamic_index_in_dim(stack, patch, axis, keepdims=False)

    first_rows = jnp.where(
        segment == 0,
        pick_patch(perturbed_frame_activation, tile_arrival_permutation[0], 0),
        inbound_activation[0],
    )
    entry_rows = [first_rows[None]]
    for turn in range(1, patch_count):
        entry_rows.append(pick_patch(perturbed_frame_activation, tile_arrival_permutation[turn], 0)[None])
    other_patch = tile_arrival_permutation[jnp.mod(1 - segment, patch_count)]
    far_k = pick_patch(earlier_step_lookup_matrix[0], other_patch, 1)
    far_v = pick_patch(earlier_step_content_matrix[0], other_patch, 1)
    packed = jnp.concatenate(entry_rows + [far_k, far_v], axis=0)
    whole = lax.all_gather(packed, "ctx", axis=1, tiled=True)
    params = [
        adaptive_shifting[0],
        adaptive_scaling[0],
        tier_query_factor[0],
        tier_skip_coefficient[0],
    ]
    first_segment = (segment == 0).astype(jnp.int32)

    def flags(tier):
        return jnp.stack([(layers_here > tier).astype(jnp.int32), first_segment])

    def own_rows(state):
        return lax.dynamic_slice_in_dim(state, place * rows, rows, 0)

    outcomes = []
    source = (whole, 0)
    turn_zero_kv = []
    for tier in range(slot_count):
        state, fresh_key, fresh_value = fused_layer(
            flags(tier),
            source,
            params,
            tier,
            (whole, patch_count + tier),
            (whole, patch_count + slot_count + tier),
        )
        source = (state[None], 0)
        turn_zero_kv.append(((fresh_key[None], 0), (fresh_value[None], 0)))
    outcomes.append(own_rows(state))
    count = lax.axis_size("segment")
    for turn in range(1, patch_count):
        core = jnp.mod(place, 2)
        half = state.shape[0] // 2
        sent = lax.dynamic_slice_in_dim(state, core * half, half, 0)
        got = lax.ppermute(sent, "segment", [(i, i + 1) for i in range(count - 1)])
        ctx_count = lax.axis_size("ctx")
        swapped = lax.ppermute(got, "ctx", [(c, c ^ 1) for c in range(ctx_count)])
        arrived = jnp.where(
            core == 0,
            jnp.concatenate([got, swapped], axis=0),
            jnp.concatenate([swapped, got], axis=0),
        )
        source = (arrived[None], 0)
        entry = (whole, turn)
        for tier in range(slot_count):
            state, _, _ = fused_layer(
                flags(tier), source, params, tier, *turn_zero_kv[tier], entry=entry, keep_kv=False
            )
            source = (state[None], 0)
            entry = None
        outcomes.append(own_rows(state))
    return jnp.stack(outcomes)[None]


def solution(mesh):
    return jax.shard_map(
        per_device,
        mesh=mesh,
        in_specs=(
            P(None, "ctx", None),
            P("segment", "ctx", None),
            P("segment"),
            P(),
            P("segment", None, None),
            P("segment", None, None),
            P("segment", None, None),
            P("segment", None, None),
            P("segment", None, None, "ctx", None),
            P("segment", None, None, "ctx", None),
        ),
        out_specs=P("segment", None, "ctx", None),
        check_vma=False,
    )
```

```python
import functools
import math

import jax
import jax.numpy as jnp
from jax import lax
from jax.experimental import pallas as pl
from jax.experimental.pallas import tpu as pltpu
from jax.sharding import PartitionSpec as P

HD = 128
EPSILON = 1e-06


def head_norm(values):
    return values * lax.rsqrt(jnp.mean(values * values, axis=-1, keepdims=True) + EPSILON)


def layer_kernel(flags_ref, *refs, two_sources, keep_kv):
    if two_sources:
        full_ref, x_ref, entry_full_ref, entry_x_ref, *refs = refs
    else:
        full_ref, x_ref, *refs = refs
    shift_ref, stretch_ref, factor_ref, skip_ref, kf_ref, vf_ref, o_ref, *kv_refs = refs
    live = flags_ref[0] > 0
    scale = 1.0 / math.sqrt(HD)
    dims = (((1,), (1,)), ((), ()))
    whole = full_ref[...]
    state = x_ref[...]
    if two_sources:
        use_entry = flags_ref[1] > 0
        whole = jnp.where(use_entry, entry_full_ref[...], whole)
        state = jnp.where(use_entry, entry_x_ref[...], state)
    whole = whole.astype(jnp.float32)
    row_scale = lax.rsqrt(jnp.mean(whole * whole, axis=-1, keepdims=True) + EPSILON)
    for j in range(state.shape[1] // HD):
        cols = slice(j * HD, (j + 1) * HD)
        x_rounded = state[:, cols]
        x = x_rounded.astype(jnp.float32)
        hidden = x * row_scale * (1.0 + stretch_ref[:, cols]) + shift_ref[:, cols]
        query = head_norm(hidden).astype(jnp.bfloat16)
        fresh_key = head_norm(hidden * factor_ref[:, cols]).astype(jnp.bfloat16)
        fresh_value = hidden.astype(jnp.bfloat16)
        if keep_kv:
            kv_refs[0][:, cols] = fresh_key
            kv_refs[1][:, cols] = fresh_value
        near = lax.dot_general(query, fresh_key, dims, preferred_element_type=jnp.float32) * scale
        far = lax.dot_general(query, kf_ref[:, cols], dims, preferred_element_type=jnp.float32) * scale
        near = jnp.exp(near)
        far = jnp.exp(far)
        total = jnp.sum(near, axis=-1, keepdims=True) + jnp.sum(far, axis=-1, keepdims=True)
        numerator = jnp.dot(
            near.astype(jnp.bfloat16), fresh_value, preferred_element_type=jnp.float32
        ) + jnp.dot(far.astype(jnp.bfloat16), vf_ref[:, cols], preferred_element_type=jnp.float32)
        attended = numerator / total
        new_state = (x + skip_ref[:, cols] * attended).astype(o_ref.dtype)
        o_ref[:, cols] = jnp.where(live, new_state, x_rounded)


def fused_layer(flags, source, params, tier, far_k, far_v, entry=None, keep_kv=True, block=1536):
    array, slab = source
    _, tokens, width = array.shape

    def slab_specs(slab_index):
        return [
            pl.BlockSpec((None, tokens, width), lambda i, f: (slab_index, 0, 0)),
            pl.BlockSpec((None, tokens, block), lambda i, f: (slab_index, 0, i)),
        ]

    def tile_of(slab_index):
        return pl.BlockSpec((None, tokens, block), lambda i, f: (slab_index, 0, i))

    line = pl.BlockSpec((None, 1, block), lambda i, f: (tier, 0, i))
    in_specs = slab_specs(slab)
    operands = [array, array]
    if entry is not None:
        in_specs += slab_specs(entry[1])
        operands += [entry[0], entry[0]]
    in_specs += [line] * 4 + [tile_of(far_k[1]), tile_of(far_v[1])]
    operands += [p.reshape(p.shape[0], 1, width) for p in params] + [far_k[0], far_v[0]]
    out_tile = pl.BlockSpec((tokens, block), lambda i, f: (0, i))
    out = jax.ShapeDtypeStruct((tokens, width), jnp.bfloat16)
    count = 3 if keep_kv else 1
    results = pl.pallas_call(
        functools.partial(layer_kernel, two_sources=entry is not None, keep_kv=keep_kv),
        out_shape=(out,) * count,
        grid_spec=pltpu.PrefetchScalarGridSpec(
            num_scalar_prefetch=1,
            grid=(width // block,),
            in_specs=in_specs,
            out_specs=(out_tile,) * count,
        ),
        cost_estimate=pl.CostEstimate(
            flops=8 * tokens * 2 * tokens * width,
            transcendentals=tokens * 2 * tokens * (width // HD),
            bytes_accessed=(4 + 2 * count) * tokens * width,
        ),
    )(flags, *operands)
    return results if keep_kv else (results[0], None, None)


def per_device(
    perturbed_frame_activation,
    inbound_activation,
    section_block_indices,
    tile_arrival_permutation,
    adaptive_shifting,
    adaptive_scaling,
    tier_query_factor,
    tier_skip_coefficient,
    earlier_step_lookup_matrix,
    earlier_step_content_matrix,
):
    segment = lax.axis_index("segment")
    place = lax.axis_index("ctx")
    patch_count = tile_arrival_permutation.shape[0]
    rows = inbound_activation.shape[1]
    width = inbound_activation.shape[2]
    slot_count = earlier_step_lookup_matrix.shape[1]
    layers_here = section_block_indices[0]

    def pick_patch(stack, patch, axis):
        chosen = lax.index_in_dim(stack, 0, axis, keepdims=False)
        for other in range(1, stack.shape[axis]):
            chosen = jnp.where(patch == other, lax.index_in_dim(stack, other, axis, keepdims=False), chosen)
        return chosen

    def arrival(position):
        chosen = tile_arrival_permutation[0]
        for index in range(1, patch_count):
            chosen = jnp.where(position == index, tile_arrival_permutation[index], chosen)
        return chosen

    first_rows = jnp.where(
        segment == 0,
        pick_patch(perturbed_frame_activation, tile_arrival_permutation[0], 0),
        inbound_activation[0],
    )
    entry_rows = [first_rows[None]]
    for turn in range(1, patch_count):
        entry_rows.append(pick_patch(perturbed_frame_activation, tile_arrival_permutation[turn], 0)[None])
    other_patch = arrival(jnp.mod(1 - segment, patch_count))
    far_k = pick_patch(earlier_step_lookup_matrix[0], other_patch, 1)
    far_v = pick_patch(earlier_step_content_matrix[0], other_patch, 1)
    packed = jnp.concatenate(entry_rows + [far_k, far_v], axis=0)
    whole = lax.all_gather(packed, "ctx", axis=1, tiled=True)
    params = [
        adaptive_shifting[0],
        adaptive_scaling[0],
        tier_query_factor[0],
        tier_skip_coefficient[0],
    ]
    first_segment = (segment == 0).astype(jnp.int32)

    def flags(tier):
        return jnp.stack([(layers_here > tier).astype(jnp.int32), first_segment])

    def own_rows(state):
        return lax.dynamic_slice_in_dim(state, place * rows, rows, 0)

    outcomes = []
    source = (whole, 0)
    turn_zero_kv = []
    for tier in range(slot_count):
        state, fresh_key, fresh_value = fused_layer(
            flags(tier),
            source,
            params,
            tier,
            (whole, patch_count + tier),
            (whole, patch_count + slot_count + tier),
        )
        source = (state[None], 0)
        turn_zero_kv.append(((fresh_key[None], 0), (fresh_value[None], 0)))
    outcomes.append(own_rows(state))
    count = lax.axis_size("segment")
    for turn in range(1, patch_count):
        core = jnp.mod(place, 2)
        half = state.shape[0] // 2
        sent = lax.dynamic_slice_in_dim(state, core * half, half, 0)
        got = lax.ppermute(sent, "segment", [(i, i + 1) for i in range(count - 1)])
        ctx_count = lax.axis_size("ctx")
        swapped = lax.ppermute(got, "ctx", [(c, c ^ 1) for c in range(ctx_count)])
        arrived = jnp.where(
            core == 0,
            jnp.concatenate([got, swapped], axis=0),
            jnp.concatenate([swapped, got], axis=0),
        )
        source = (arrived[None], 0)
        entry = (whole, turn)
        for tier in range(slot_count):
            state, _, _ = fused_layer(
                flags(tier), source, params, tier, *turn_zero_kv[tier], entry=entry, keep_kv=False
            )
            source = (state[None], 0)
            entry = None
        outcomes.append(own_rows(state))
    return jnp.stack(outcomes)[None]


def solution(mesh):
    return jax.shard_map(
        per_device,
        mesh=mesh,
        in_specs=(
            P(None, "ctx", None),
            P("segment", "ctx", None),
            P("segment"),
            P(),
            P("segment", None, None),
            P("segment", None, None),
            P("segment", None, None),
            P("segment", None, None),
            P("segment", None, None, "ctx", None),
            P("segment", None, None, "ctx", None),
        ),
        out_specs=P("segment", None, "ctx", None),
        check_vma=False,
    )
```

```python
import functools
import math

import jax
import jax.numpy as jnp
from jax import lax
from jax.experimental import pallas as pl
from jax.experimental.pallas import tpu as pltpu
from jax.sharding import PartitionSpec as P

HD = 128
EPSILON = 1e-06


def head_norm(values):
    return values * lax.rsqrt(jnp.mean(values * values, axis=-1, keepdims=True) + EPSILON)


def layer_kernel(flags_ref, *refs, two_sources, keep_kv, query_rows):
    if two_sources:
        full_ref, x_ref, entry_full_ref, entry_x_ref, *refs = refs
    else:
        full_ref, x_ref, *refs = refs
    shift_ref, stretch_ref, factor_ref, skip_ref, kf_ref, vf_ref, o_ref, *kv_refs = refs
    live = flags_ref[0] > 0
    scale = 1.0 / math.sqrt(HD)
    dims = (((1,), (1,)), ((), ()))
    whole = full_ref[...]
    state = x_ref[...]
    if two_sources:
        use_entry = flags_ref[1] > 0
        whole = jnp.where(use_entry, entry_full_ref[...], whole)
        state = jnp.where(use_entry, entry_x_ref[...], state)
    def row_scale_of(rows_value):
        rows_value = rows_value.astype(jnp.float32)
        return lax.rsqrt(jnp.mean(rows_value * rows_value, axis=-1, keepdims=True) + EPSILON)

    row_scale = row_scale_of(whole)
    if query_rows is None:
        state_q, row_scale_q = state, row_scale
    else:
        start = pl.multiple_of(flags_ref[2], query_rows)
        state_q = x_ref[pl.ds(start, query_rows), :]
        row_scale_q = row_scale_of(full_ref[pl.ds(start, query_rows), :])
    for j in range(state.shape[1] // HD):
        cols = slice(j * HD, (j + 1) * HD)
        stretch = 1.0 + stretch_ref[:, cols]
        x_all = state[:, cols].astype(jnp.float32)
        hidden = x_all * row_scale * stretch + shift_ref[:, cols]
        fresh_key = head_norm(hidden * factor_ref[:, cols]).astype(jnp.bfloat16)
        fresh_value = hidden.astype(jnp.bfloat16)
        x_rounded = state_q[:, cols]
        x = x_rounded.astype(jnp.float32)
        if query_rows is not None:
            hidden = x * row_scale_q * stretch + shift_ref[:, cols]
        query = head_norm(hidden).astype(jnp.bfloat16)
        if keep_kv:
            kv_refs[0][:, cols] = fresh_key
            kv_refs[1][:, cols] = fresh_value
        near = lax.dot_general(query, fresh_key, dims, preferred_element_type=jnp.float32) * scale
        far = lax.dot_general(query, kf_ref[:, cols], dims, preferred_element_type=jnp.float32) * scale
        near = jnp.exp(near)
        far = jnp.exp(far)
        total = jnp.sum(near, axis=-1, keepdims=True) + jnp.sum(far, axis=-1, keepdims=True)
        numerator = jnp.dot(
            near.astype(jnp.bfloat16), fresh_value, preferred_element_type=jnp.float32
        ) + jnp.dot(far.astype(jnp.bfloat16), vf_ref[:, cols], preferred_element_type=jnp.float32)
        attended = numerator / total
        new_state = (x + skip_ref[:, cols] * attended).astype(o_ref.dtype)
        o_ref[:, cols] = jnp.where(live, new_state, x_rounded)


def fused_layer(
    flags, source, params, tier, far_k, far_v, entry=None, keep_kv=True, query_rows=None, block=1536
):
    array, slab = source
    _, tokens, width = array.shape

    def slab_specs(slab_index):
        return [
            pl.BlockSpec((None, tokens, width), lambda i, f: (slab_index, 0, 0)),
            pl.BlockSpec((None, tokens, block), lambda i, f: (slab_index, 0, i)),
        ]

    def tile_of(slab_index):
        return pl.BlockSpec((None, tokens, block), lambda i, f: (slab_index, 0, i))

    line = pl.BlockSpec((None, 1, block), lambda i, f: (tier, 0, i))
    in_specs = slab_specs(slab)
    operands = [array, array]
    if entry is not None:
        in_specs += slab_specs(entry[1])
        operands += [entry[0], entry[0]]
    in_specs += [line] * 4 + [tile_of(far_k[1]), tile_of(far_v[1])]
    operands += [p.reshape(p.shape[0], 1, width) for p in params] + [far_k[0], far_v[0]]
    out_tile = pl.BlockSpec((tokens, block), lambda i, f: (0, i))
    out = jax.ShapeDtypeStruct((tokens, width), jnp.bfloat16)
    count = 3 if keep_kv else 1
    out_shapes = (out,) * count
    out_specs = (out_tile,) * count
    if query_rows is not None:
        assert not keep_kv and block == width and entry is None
        out_shapes = (jax.ShapeDtypeStruct((query_rows, width), jnp.bfloat16),)
        out_specs = (pl.BlockSpec((query_rows, block), lambda i, f: (0, i)),)
    results = pl.pallas_call(
        functools.partial(
            layer_kernel, two_sources=entry is not None, keep_kv=keep_kv, query_rows=query_rows
        ),
        out_shape=out_shapes,
        grid_spec=pltpu.PrefetchScalarGridSpec(
            num_scalar_prefetch=1,
            grid=(width // block,),
            in_specs=in_specs,
            out_specs=out_specs,
        ),
        cost_estimate=pl.CostEstimate(
            flops=8 * tokens * 2 * tokens * width,
            transcendentals=tokens * 2 * tokens * (width // HD),
            bytes_accessed=(4 + 2 * count) * tokens * width,
        ),
    )(flags, *operands)
    return results if keep_kv else (results[0], None, None)


def per_device(
    perturbed_frame_activation,
    inbound_activation,
    section_block_indices,
    tile_arrival_permutation,
    adaptive_shifting,
    adaptive_scaling,
    tier_query_factor,
    tier_skip_coefficient,
    earlier_step_lookup_matrix,
    earlier_step_content_matrix,
):
    segment = lax.axis_index("segment")
    place = lax.axis_index("ctx")
    patch_count = tile_arrival_permutation.shape[0]
    rows = inbound_activation.shape[1]
    width = inbound_activation.shape[2]
    slot_count = earlier_step_lookup_matrix.shape[1]
    layers_here = section_block_indices[0]

    def pick_patch(stack, patch, axis):
        chosen = lax.index_in_dim(stack, 0, axis, keepdims=False)
        for other in range(1, stack.shape[axis]):
            chosen = jnp.where(patch == other, lax.index_in_dim(stack, other, axis, keepdims=False), chosen)
        return chosen

    def arrival(position):
        chosen = tile_arrival_permutation[0]
        for index in range(1, patch_count):
            chosen = jnp.where(position == index, tile_arrival_permutation[index], chosen)
        return chosen

    first_rows = jnp.where(
        segment == 0,
        pick_patch(perturbed_frame_activation, tile_arrival_permutation[0], 0),
        inbound_activation[0],
    )
    entry_rows = [first_rows[None]]
    for turn in range(1, patch_count):
        entry_rows.append(pick_patch(perturbed_frame_activation, tile_arrival_permutation[turn], 0)[None])
    other_patch = arrival(jnp.mod(1 - segment, patch_count))
    far_k = pick_patch(earlier_step_lookup_matrix[0], other_patch, 1)
    far_v = pick_patch(earlier_step_content_matrix[0], other_patch, 1)
    packed = jnp.concatenate(entry_rows + [far_k, far_v], axis=0)
    whole = lax.all_gather(packed, "ctx", axis=1, tiled=True)
    params = [
        adaptive_shifting[0],
        adaptive_scaling[0],
        tier_query_factor[0],
        tier_skip_coefficient[0],
    ]
    first_segment = (segment == 0).astype(jnp.int32)

    def flags(tier):
        live = (layers_here > tier).astype(jnp.int32)
        return jnp.stack([live, first_segment, (place * rows).astype(jnp.int32)])

    def own_rows(state):
        return lax.dynamic_slice_in_dim(state, place * rows, rows, 0)

    outcomes = []
    source = (whole, 0)
    turn_zero_kv = []
    for tier in range(slot_count):
        state, fresh_key, fresh_value = fused_layer(
            flags(tier),
            source,
            params,
            tier,
            (whole, patch_count + tier),
            (whole, patch_count + slot_count + tier),
        )
        source = (state[None], 0)
        turn_zero_kv.append(((fresh_key[None], 0), (fresh_value[None], 0)))
    outcomes.append(own_rows(state))
    count = lax.axis_size("segment")
    for turn in range(1, patch_count):
        core = jnp.mod(place, 2)
        half = state.shape[0] // 2
        sent = lax.dynamic_slice_in_dim(state, core * half, half, 0)
        got = lax.ppermute(sent, "segment", [(i, i + 1) for i in range(count - 1)])
        ctx_count = lax.axis_size("ctx")
        swapped = lax.ppermute(got, "ctx", [(c, c ^ 1) for c in range(ctx_count)])
        arrived = jnp.where(
            core == 0,
            jnp.concatenate([got, swapped], axis=0),
            jnp.concatenate([swapped, got], axis=0),
        )
        source = (arrived[None], 0)
        entry = (whole, turn)
        for tier in range(slot_count):
            last = turn == patch_count - 1 and tier == slot_count - 1
            state, _, _ = fused_layer(
                flags(tier),
                source,
                params,
                tier,
                *turn_zero_kv[tier],
                entry=entry,
                keep_kv=False,
                query_rows=rows if last else None,
            )
            source = (state[None], 0)
            entry = None
        outcomes.append(state if state.shape[0] == rows else own_rows(state))
    return jnp.stack(outcomes)[None]


def solution(mesh):
    return jax.shard_map(
        per_device,
        mesh=mesh,
        in_specs=(
            P(None, "ctx", None),
            P("segment", "ctx", None),
            P("segment"),
            P(),
            P("segment", None, None),
            P("segment", None, None),
            P("segment", None, None),
            P("segment", None, None),
            P("segment", None, None, "ctx", None),
            P("segment", None, None, "ctx", None),
        ),
        out_specs=P("segment", None, "ctx", None),
        check_vma=False,
    )
```

```python
import functools
import math

import jax
import jax.numpy as jnp
from jax import lax
from jax.experimental import pallas as pl
from jax.experimental.pallas import tpu as pltpu
from jax.sharding import PartitionSpec as P

HD = 128
EPSILON = 1e-06


def head_norm(values):
    return values * lax.rsqrt(jnp.mean(values * values, axis=-1, keepdims=True) + EPSILON)


def layer_kernel(flags_ref, *refs, two_sources, keep_kv, query_rows):
    if two_sources:
        full_ref, entry_full_ref, *refs = refs
        entry_x_ref = entry_full_ref
    else:
        full_ref, *refs = refs
    x_ref = full_ref
    shift_ref, stretch_ref, factor_ref, skip_ref, kf_ref, vf_ref, o_ref, *kv_refs = refs
    live = flags_ref[0] > 0
    scale = 1.0 / math.sqrt(HD)
    dims = (((1,), (1,)), ((), ()))
    whole = full_ref[...]
    state = x_ref[...]
    if two_sources:
        use_entry = flags_ref[1] > 0
        whole = jnp.where(use_entry, entry_full_ref[...], whole)
        state = jnp.where(use_entry, entry_x_ref[...], state)
    def row_scale_of(rows_value):
        rows_value = rows_value.astype(jnp.float32)
        return lax.rsqrt(jnp.mean(rows_value * rows_value, axis=-1, keepdims=True) + EPSILON)

    row_scale = row_scale_of(whole)
    if query_rows is None:
        state_q, row_scale_q = state, row_scale
    else:
        start = pl.multiple_of(flags_ref[2], query_rows)
        state_q = x_ref[pl.ds(start, query_rows), :]
        row_scale_q = row_scale_of(full_ref[pl.ds(start, query_rows), :])
    for j in range(state.shape[1] // HD):
        cols = slice(j * HD, (j + 1) * HD)
        stretch = 1.0 + stretch_ref[:, cols]
        x_all = state[:, cols].astype(jnp.float32)
        hidden = x_all * row_scale * stretch + shift_ref[:, cols]
        fresh_key = head_norm(hidden * factor_ref[:, cols]).astype(jnp.bfloat16)
        fresh_value = hidden.astype(jnp.bfloat16)
        x_rounded = state_q[:, cols]
        x = x_rounded.astype(jnp.float32)
        if query_rows is not None:
            hidden = x * row_scale_q * stretch + shift_ref[:, cols]
        query = head_norm(hidden).astype(jnp.bfloat16)
        if keep_kv:
            kv_refs[0][:, cols] = fresh_key
            kv_refs[1][:, cols] = fresh_value
        near = lax.dot_general(query, fresh_key, dims, preferred_element_type=jnp.float32) * scale
        far = lax.dot_general(query, kf_ref[:, cols], dims, preferred_element_type=jnp.float32) * scale
        near = jnp.exp(near)
        far = jnp.exp(far)
        total = jnp.sum(near, axis=-1, keepdims=True) + jnp.sum(far, axis=-1, keepdims=True)
        numerator = jnp.dot(
            near.astype(jnp.bfloat16), fresh_value, preferred_element_type=jnp.float32
        ) + jnp.dot(far.astype(jnp.bfloat16), vf_ref[:, cols], preferred_element_type=jnp.float32)
        attended = numerator / total
        new_state = (x + skip_ref[:, cols] * attended).astype(o_ref.dtype)
        o_ref[:, cols] = jnp.where(live, new_state, x_rounded)


def fused_layer(flags, source, params, tier, far_k, far_v, entry=None, keep_kv=True, query_rows=None):
    array, slab = source
    _, tokens, width = array.shape
    block = width

    def slab_specs(slab_index):
        return [pl.BlockSpec((None, tokens, width), lambda i, f: (slab_index, 0, 0))]

    def tile_of(slab_index):
        return pl.BlockSpec((None, tokens, block), lambda i, f: (slab_index, 0, i))

    line = pl.BlockSpec((None, 1, block), lambda i, f: (tier, 0, i))
    in_specs = slab_specs(slab)
    operands = [array]
    if entry is not None:
        in_specs += slab_specs(entry[1])
        operands += [entry[0]]
    in_specs += [line] * 4 + [tile_of(far_k[1]), tile_of(far_v[1])]
    operands += [p.reshape(p.shape[0], 1, width) for p in params] + [far_k[0], far_v[0]]
    out_tile = pl.BlockSpec((tokens, block), lambda i, f: (0, i))
    out = jax.ShapeDtypeStruct((tokens, width), jnp.bfloat16)
    count = 3 if keep_kv else 1
    out_shapes = (out,) * count
    out_specs = (out_tile,) * count
    if query_rows is not None:
        assert not keep_kv and entry is None
        out_shapes = (jax.ShapeDtypeStruct((query_rows, width), jnp.bfloat16),)
        out_specs = (pl.BlockSpec((query_rows, block), lambda i, f: (0, i)),)
    results = pl.pallas_call(
        functools.partial(
            layer_kernel, two_sources=entry is not None, keep_kv=keep_kv, query_rows=query_rows
        ),
        out_shape=out_shapes,
        grid_spec=pltpu.PrefetchScalarGridSpec(
            num_scalar_prefetch=1,
            grid=(width // block,),
            in_specs=in_specs,
            out_specs=out_specs,
        ),
        cost_estimate=pl.CostEstimate(
            flops=8 * tokens * 2 * tokens * width,
            transcendentals=tokens * 2 * tokens * (width // HD),
            bytes_accessed=(4 + 2 * count) * tokens * width,
        ),
    )(flags, *operands)
    return results if keep_kv else (results[0], None, None)


def per_device(
    perturbed_frame_activation,
    inbound_activation,
    section_block_indices,
    tile_arrival_permutation,
    adaptive_shifting,
    adaptive_scaling,
    tier_query_factor,
    tier_skip_coefficient,
    earlier_step_lookup_matrix,
    earlier_step_content_matrix,
):
    segment = lax.axis_index("segment")
    place = lax.axis_index("ctx")
    patch_count = tile_arrival_permutation.shape[0]
    rows = inbound_activation.shape[1]
    width = inbound_activation.shape[2]
    slot_count = earlier_step_lookup_matrix.shape[1]
    layers_here = section_block_indices[0]

    def pick_patch(stack, patch, axis):
        chosen = lax.index_in_dim(stack, 0, axis, keepdims=False)
        for other in range(1, stack.shape[axis]):
            chosen = jnp.where(patch == other, lax.index_in_dim(stack, other, axis, keepdims=False), chosen)
        return chosen

    def arrival(position):
        chosen = tile_arrival_permutation[0]
        for index in range(1, patch_count):
            chosen = jnp.where(position == index, tile_arrival_permutation[index], chosen)
        return chosen

    first_rows = jnp.where(
        segment == 0,
        pick_patch(perturbed_frame_activation, tile_arrival_permutation[0], 0),
        inbound_activation[0],
    )
    entry_rows = [first_rows[None]]
    for turn in range(1, patch_count):
        entry_rows.append(pick_patch(perturbed_frame_activation, tile_arrival_permutation[turn], 0)[None])
    other_patch = arrival(jnp.mod(1 - segment, patch_count))
    far_k = pick_patch(earlier_step_lookup_matrix[0], other_patch, 1)
    far_v = pick_patch(earlier_step_content_matrix[0], other_patch, 1)
    packed = jnp.concatenate(entry_rows + [far_k, far_v], axis=0)
    whole = lax.all_gather(packed, "ctx", axis=1, tiled=True)
    params = [
        adaptive_shifting[0],
        adaptive_scaling[0],
        tier_query_factor[0],
        tier_skip_coefficient[0],
    ]
    first_segment = (segment == 0).astype(jnp.int32)

    def flags(tier):
        live = (layers_here > tier).astype(jnp.int32)
        return jnp.stack([live, first_segment, (place * rows).astype(jnp.int32)])

    def own_rows(state):
        return lax.dynamic_slice_in_dim(state, place * rows, rows, 0)

    outcomes = []
    source = (whole, 0)
    turn_zero_kv = []
    for tier in range(slot_count):
        state, fresh_key, fresh_value = fused_layer(
            flags(tier),
            source,
            params,
            tier,
            (whole, patch_count + tier),
            (whole, patch_count + slot_count + tier),
        )
        source = (state[None], 0)
        turn_zero_kv.append(((fresh_key[None], 0), (fresh_value[None], 0)))
    outcomes.append(own_rows(state))
    count = lax.axis_size("segment")
    for turn in range(1, patch_count):
        core = jnp.mod(place, 2)
        half = state.shape[0] // 2
        sent = lax.dynamic_slice_in_dim(state, core * half, half, 0)
        got = lax.ppermute(sent, "segment", [(i, i + 1) for i in range(count - 1)])
        ctx_count = lax.axis_size("ctx")
        swapped = lax.ppermute(got, "ctx", [(c, c ^ 1) for c in range(ctx_count)])
        arrived = jnp.where(
            core == 0,
            jnp.concatenate([got, swapped], axis=0),
            jnp.concatenate([swapped, got], axis=0),
        )
        source = (arrived[None], 0)
        entry = (whole, turn)
        for tier in range(slot_count):
            last = turn == patch_count - 1 and tier == slot_count - 1
            state, _, _ = fused_layer(
                flags(tier),
                source,
                params,
                tier,
                *turn_zero_kv[tier],
                entry=entry,
                keep_kv=False,
                query_rows=rows if last else None,
            )
            source = (state[None], 0)
            entry = None
        outcomes.append(state if state.shape[0] == rows else own_rows(state))
    return jnp.stack(outcomes)[None]


def solution(mesh):
    return jax.shard_map(
        per_device,
        mesh=mesh,
        in_specs=(
            P(None, "ctx", None),
            P("segment", "ctx", None),
            P("segment"),
            P(),
            P("segment", None, None),
            P("segment", None, None),
            P("segment", None, None),
            P("segment", None, None),
            P("segment", None, None, "ctx", None),
            P("segment", None, None, "ctx", None),
        ),
        out_specs=P("segment", None, "ctx", None),
        check_vma=False,
    )
```

```python
import functools
import math

import jax
import jax.numpy as jnp
from jax import lax
from jax.experimental import pallas as pl
from jax.experimental.pallas import tpu as pltpu
from jax.sharding import PartitionSpec as P

HD = 128
EPSILON = 1e-06


def head_norm(values):
    return values * lax.rsqrt(jnp.mean(values * values, axis=-1, keepdims=True) + EPSILON)


def layer_kernel(flags_ref, *refs, two_sources, keep_kv, query_rows, emit_rows, aliased):
    if two_sources:
        full_ref, entry_full_ref, *refs = refs
        entry_x_ref = entry_full_ref
    else:
        full_ref, *refs = refs
    x_ref = full_ref
    shift_ref, stretch_ref, factor_ref, skip_ref, kf_ref, vf_ref, *refs = refs
    if aliased:
        refs = refs[1:]
    o_ref, *refs = refs
    kv_refs = refs[:2] if keep_kv else ()
    live = flags_ref[0] > 0
    scale = 1.0 / math.sqrt(HD)
    dims = (((1,), (1,)), ((), ()))
    whole = full_ref[...]
    state = x_ref[...]
    if two_sources:
        use_entry = flags_ref[1] > 0
        whole = jnp.where(use_entry, entry_full_ref[...], whole)
        state = jnp.where(use_entry, entry_x_ref[...], state)
    def row_scale_of(rows_value):
        rows_value = rows_value.astype(jnp.float32)
        return lax.rsqrt(jnp.mean(rows_value * rows_value, axis=-1, keepdims=True) + EPSILON)

    row_scale = row_scale_of(whole)
    if query_rows is None:
        state_q, row_scale_q = state, row_scale
    else:
        start = pl.multiple_of(flags_ref[2], query_rows)
        state_q = x_ref[pl.ds(start, query_rows), :]
        row_scale_q = row_scale_of(full_ref[pl.ds(start, query_rows), :])
    for j in range(state.shape[1] // HD):
        cols = slice(j * HD, (j + 1) * HD)
        stretch = 1.0 + stretch_ref[:, cols]
        x_all = state[:, cols].astype(jnp.float32)
        hidden = x_all * row_scale * stretch + shift_ref[:, cols]
        fresh_key = head_norm(hidden * factor_ref[:, cols]).astype(jnp.bfloat16)
        fresh_value = hidden.astype(jnp.bfloat16)
        x_rounded = state_q[:, cols]
        x = x_rounded.astype(jnp.float32)
        if query_rows is not None:
            hidden = x * row_scale_q * stretch + shift_ref[:, cols]
        query = head_norm(hidden).astype(jnp.bfloat16)
        if keep_kv:
            kv_refs[0][:, cols] = fresh_key
            kv_refs[1][:, cols] = fresh_value
        near = lax.dot_general(query, fresh_key, dims, preferred_element_type=jnp.float32) * scale
        far = lax.dot_general(query, kf_ref[:, cols], dims, preferred_element_type=jnp.float32) * scale
        near = jnp.exp(near)
        far = jnp.exp(far)
        total = jnp.sum(near, axis=-1, keepdims=True) + jnp.sum(far, axis=-1, keepdims=True)
        numerator = jnp.dot(
            near.astype(jnp.bfloat16), fresh_value, preferred_element_type=jnp.float32
        ) + jnp.dot(far.astype(jnp.bfloat16), vf_ref[:, cols], preferred_element_type=jnp.float32)
        attended = numerator / total
        new_state = (x + skip_ref[:, cols] * attended).astype(o_ref.dtype)
        o_ref[:, cols] = jnp.where(live, new_state, x_rounded)
    if emit_rows:
        half_ref, rows_ref = refs[len(kv_refs) :]
        half = half_ref.shape[0]
        rows = rows_ref.shape[0]
        half_ref[...] = o_ref[pl.ds(pl.multiple_of(flags_ref[3], half), half), :]
        rows_ref[...] = o_ref[pl.ds(pl.multiple_of(flags_ref[2], rows), rows), :]


def fused_layer(
    flags,
    source,
    params,
    tier,
    far_k,
    far_v,
    entry=None,
    keep_kv=True,
    query_rows=None,
    emit_rows=None,
    into=None,
):
    array, slab = source
    _, tokens, width = array.shape
    block = width

    def slab_specs(slab_index):
        return [pl.BlockSpec((None, tokens, width), lambda i, f: (slab_index, 0, 0))]

    def tile_of(slab_index):
        return pl.BlockSpec((None, tokens, block), lambda i, f: (slab_index, 0, i))

    line = pl.BlockSpec((None, 1, block), lambda i, f: (tier, 0, i))
    in_specs = slab_specs(slab)
    operands = [array]
    if entry is not None:
        in_specs += slab_specs(entry[1])
        operands += [entry[0]]
    in_specs += [line] * 4 + [tile_of(far_k[1]), tile_of(far_v[1])]
    operands += [p.reshape(p.shape[0], 1, width) for p in params] + [far_k[0], far_v[0]]
    aliases = {}
    out_tile = pl.BlockSpec((tokens, block), lambda i, f: (0, i))
    out = jax.ShapeDtypeStruct((tokens, width), jnp.bfloat16)
    count = 3 if keep_kv else 1
    out_shapes = (out,) * count
    out_specs = (out_tile,) * count
    if query_rows is not None:
        assert not keep_kv and entry is None
        out_shapes = (jax.ShapeDtypeStruct((query_rows, width), jnp.bfloat16),)
        out_specs = (pl.BlockSpec((query_rows, block), lambda i, f: (0, i)),)
    if into is not None:
        assert query_rows is not None
        buffer, slot = into
        in_specs.append(pl.BlockSpec(memory_space=pl.ANY))
        operands.append(buffer)
        aliases = {len(operands): 0}
        out_shapes = (jax.ShapeDtypeStruct(buffer.shape, buffer.dtype),)
        out_specs = (pl.BlockSpec((None, query_rows, block), lambda i, f: (slot, 0, i)),)
    if emit_rows is not None:
        half, rows, slots = emit_rows
        out_shapes += (
            jax.ShapeDtypeStruct((half, width), jnp.bfloat16),
            jax.ShapeDtypeStruct((slots, rows, width), jnp.bfloat16),
        )
        out_specs += (
            pl.BlockSpec((half, block), lambda i, f: (0, i)),
            pl.BlockSpec((None, rows, block), lambda i, f: (0, 0, i)),
        )
    return pl.pallas_call(
        functools.partial(
            layer_kernel,
            two_sources=entry is not None,
            keep_kv=keep_kv,
            query_rows=query_rows,
            emit_rows=emit_rows is not None,
            aliased=into is not None,
        ),
        out_shape=out_shapes,
        grid_spec=pltpu.PrefetchScalarGridSpec(
            num_scalar_prefetch=1,
            grid=(width // block,),
            in_specs=in_specs,
            out_specs=out_specs,
        ),
        input_output_aliases=aliases,
        cost_estimate=pl.CostEstimate(
            flops=8 * tokens * 2 * tokens * width,
            transcendentals=tokens * 2 * tokens * (width // HD),
            bytes_accessed=(4 + 2 * count) * tokens * width,
        ),
    )(flags, *operands)


def per_device(
    perturbed_frame_activation,
    inbound_activation,
    section_block_indices,
    tile_arrival_permutation,
    adaptive_shifting,
    adaptive_scaling,
    tier_query_factor,
    tier_skip_coefficient,
    earlier_step_lookup_matrix,
    earlier_step_content_matrix,
):
    segment = lax.axis_index("segment")
    place = lax.axis_index("ctx")
    patch_count = tile_arrival_permutation.shape[0]
    rows = inbound_activation.shape[1]
    width = inbound_activation.shape[2]
    slot_count = earlier_step_lookup_matrix.shape[1]
    layers_here = section_block_indices[0]

    def pick_patch(stack, patch, axis):
        chosen = lax.index_in_dim(stack, 0, axis, keepdims=False)
        for other in range(1, stack.shape[axis]):
            chosen = jnp.where(patch == other, lax.index_in_dim(stack, other, axis, keepdims=False), chosen)
        return chosen

    def arrival(position):
        chosen = tile_arrival_permutation[0]
        for index in range(1, patch_count):
            chosen = jnp.where(position == index, tile_arrival_permutation[index], chosen)
        return chosen

    first_rows = jnp.where(
        segment == 0,
        pick_patch(perturbed_frame_activation, tile_arrival_permutation[0], 0),
        inbound_activation[0],
    )
    entry_rows = [first_rows[None]]
    for turn in range(1, patch_count):
        entry_rows.append(pick_patch(perturbed_frame_activation, tile_arrival_permutation[turn], 0)[None])
    other_patch = arrival(jnp.mod(1 - segment, patch_count))
    far_k = pick_patch(earlier_step_lookup_matrix[0], other_patch, 1)
    far_v = pick_patch(earlier_step_content_matrix[0], other_patch, 1)
    packed = jnp.concatenate(entry_rows + [far_k, far_v], axis=0)
    whole = lax.all_gather(packed, "ctx", axis=1, tiled=True)
    params = [
        adaptive_shifting[0],
        adaptive_scaling[0],
        tier_query_factor[0],
        tier_skip_coefficient[0],
    ]
    first_segment = (segment == 0).astype(jnp.int32)
    core = jnp.mod(place, 2)
    half = rows * lax.axis_size("ctx") // 2

    def flags(tier):
        live = (layers_here > tier).astype(jnp.int32)
        return jnp.stack([live, first_segment, (place * rows).astype(jnp.int32), (core * half).astype(jnp.int32)])

    source = (whole, 0)
    turn_zero_kv = []
    for tier in range(slot_count):
        last = tier == slot_count - 1
        results = fused_layer(
            flags(tier),
            source,
            params,
            tier,
            (whole, patch_count + tier),
            (whole, patch_count + slot_count + tier),
            emit_rows=(half, rows, patch_count) if last else None,
        )
        state, fresh_key, fresh_value = results[:3]
        source = (state[None], 0)
        turn_zero_kv.append(((fresh_key[None], 0), (fresh_value[None], 0)))
    sent, outcomes = results[3:]
    count = lax.axis_size("segment")
    for turn in range(1, patch_count):
        got = lax.ppermute(sent, "segment", [(i, i + 1) for i in range(count - 1)])
        ctx_count = lax.axis_size("ctx")
        swapped = lax.ppermute(got, "ctx", [(c, c ^ 1) for c in range(ctx_count)])
        arrived = jnp.where(
            core == 0,
            jnp.concatenate([got, swapped], axis=0),
            jnp.concatenate([swapped, got], axis=0),
        )
        source = (arrived[None], 0)
        entry = (whole, turn)
        for tier in range(slot_count):
            last = tier == slot_count - 1
            if last:
                assert turn == patch_count - 1
                (outcomes,) = fused_layer(
                    flags(tier),
                    source,
                    params,
                    tier,
                    *turn_zero_kv[tier],
                    keep_kv=False,
                    query_rows=rows,
                    into=(outcomes, turn),
                )
            else:
                (state,) = fused_layer(
                    flags(tier), source, params, tier, *turn_zero_kv[tier], entry=entry, keep_kv=False
                )
                source = (state[None], 0)
                entry = None
    return outcomes[None]


def solution(mesh):
    return jax.shard_map(
        per_device,
        mesh=mesh,
        in_specs=(
            P(None, "ctx", None),
            P("segment", "ctx", None),
            P("segment"),
            P(),
            P("segment", None, None),
            P("segment", None, None),
            P("segment", None, None),
            P("segment", None, None),
            P("segment", None, None, "ctx", None),
            P("segment", None, None, "ctx", None),
        ),
        out_specs=P("segment", None, "ctx", None),
        check_vma=False,
    )
```

```python
import functools
import math

import jax
import jax.numpy as jnp
from jax import lax
from jax.experimental import pallas as pl
from jax.experimental.pallas import tpu as pltpu
from jax.sharding import PartitionSpec as P

HD = 128
EPSILON = 1e-06


def head_norm(values):
    return values * lax.rsqrt(jnp.mean(values * values, axis=-1, keepdims=True) + EPSILON)


def layer_kernel(flags_ref, *refs, two_sources, keep_kv, query_rows, emit_rows, aliased, far_slabs):
    if two_sources:
        full_ref, entry_full_ref, *refs = refs
        entry_x_ref = entry_full_ref
    else:
        full_ref, *refs = refs
    x_ref = full_ref
    shift_ref, stretch_ref, factor_ref, skip_ref, kf_hbm, vf_hbm, *refs = refs
    if aliased:
        refs = refs[1:]
    o_ref, *refs = refs
    kf_ref, vf_ref, num_ref, total_ref, query_ref, copy_sems = refs[-6:]
    refs = refs[:-6]
    kv_refs = refs[:2] if keep_kv else ()
    far_copies = [
        pltpu.make_async_copy(kf_hbm.at[far_slabs[0]], kf_ref, copy_sems.at[0]),
        pltpu.make_async_copy(vf_hbm.at[far_slabs[1]], vf_ref, copy_sems.at[1]),
    ]
    for copy in far_copies:
        copy.start()
    live = flags_ref[0] > 0
    scale = 1.0 / math.sqrt(HD)
    dims = (((1,), (1,)), ((), ()))
    whole = full_ref[...]
    state = x_ref[...]
    if two_sources:
        use_entry = flags_ref[1] > 0
        whole = jnp.where(use_entry, entry_full_ref[...], whole)
        state = jnp.where(use_entry, entry_x_ref[...], state)

    def row_scale_of(rows_value):
        rows_value = rows_value.astype(jnp.float32)
        return lax.rsqrt(jnp.mean(rows_value * rows_value, axis=-1, keepdims=True) + EPSILON)

    row_scale = row_scale_of(whole)
    if query_rows is None:
        state_q, row_scale_q = state, row_scale
    else:
        start = pl.multiple_of(flags_ref[2], query_rows)
        state_q = x_ref[pl.ds(start, query_rows), :]
        row_scale_q = row_scale_of(full_ref[pl.ds(start, query_rows), :])
    heads = state.shape[1] // HD
    for j in range(heads):
        cols = slice(j * HD, (j + 1) * HD)
        stretch = 1.0 + stretch_ref[:, cols]
        x_all = state[:, cols].astype(jnp.float32)
        hidden = x_all * row_scale * stretch + shift_ref[:, cols]
        fresh_key = head_norm(hidden * factor_ref[:, cols]).astype(jnp.bfloat16)
        fresh_value = hidden.astype(jnp.bfloat16)
        if query_rows is not None:
            x = state_q[:, cols].astype(jnp.float32)
            hidden = x * row_scale_q * stretch + shift_ref[:, cols]
        query = head_norm(hidden).astype(jnp.bfloat16)
        query_ref[:, cols] = query
        if keep_kv:
            kv_refs[0][:, cols] = fresh_key
            kv_refs[1][:, cols] = fresh_value
        near = lax.dot_general(query, fresh_key, dims, preferred_element_type=jnp.float32) * scale
        near = jnp.exp(near)
        total_ref[:, cols] = jnp.broadcast_to(jnp.sum(near, axis=-1, keepdims=True), query.shape)
        num_ref[:, cols] = jnp.dot(near.astype(jnp.bfloat16), fresh_value, preferred_element_type=jnp.float32)
    for copy in far_copies:
        copy.wait()
    for j in range(heads):
        cols = slice(j * HD, (j + 1) * HD)
        query = query_ref[:, cols]
        far = lax.dot_general(query, kf_ref[:, cols], dims, preferred_element_type=jnp.float32) * scale
        far = jnp.exp(far)
        total = total_ref[:, cols][:, :1] + jnp.sum(far, axis=-1, keepdims=True)
        numerator = num_ref[:, cols] + jnp.dot(
            far.astype(jnp.bfloat16), vf_ref[:, cols], preferred_element_type=jnp.float32
        )
        attended = numerator / total
        x_rounded = state_q[:, cols]
        x = x_rounded.astype(jnp.float32)
        new_state = (x + skip_ref[:, cols] * attended).astype(o_ref.dtype)
        o_ref[:, cols] = jnp.where(live, new_state, x_rounded)
    if emit_rows:
        half_ref, rows_ref = refs[len(kv_refs) :]
        half = half_ref.shape[0]
        rows = rows_ref.shape[0]
        half_ref[...] = o_ref[pl.ds(pl.multiple_of(flags_ref[3], half), half), :]
        rows_ref[...] = o_ref[pl.ds(pl.multiple_of(flags_ref[2], rows), rows), :]


def fused_layer(
    flags,
    source,
    params,
    tier,
    far_k,
    far_v,
    entry=None,
    keep_kv=True,
    query_rows=None,
    emit_rows=None,
    into=None,
):
    array, slab = source
    _, tokens, width = array.shape
    block = width

    def slab_specs(slab_index):
        return [pl.BlockSpec((None, tokens, width), lambda i, f: (slab_index, 0, 0))]

    def tile_of(slab_index):
        return pl.BlockSpec((None, tokens, block), lambda i, f: (slab_index, 0, i))

    line = pl.BlockSpec((None, 1, block), lambda i, f: (tier, 0, i))
    in_specs = slab_specs(slab)
    operands = [array]
    if entry is not None:
        in_specs += slab_specs(entry[1])
        operands += [entry[0]]
    in_specs += [line] * 4 + [pl.BlockSpec(memory_space=pl.ANY)] * 2
    operands += [p.reshape(p.shape[0], 1, width) for p in params] + [far_k[0], far_v[0]]
    aliases = {}
    out_tile = pl.BlockSpec((tokens, block), lambda i, f: (0, i))
    out = jax.ShapeDtypeStruct((tokens, width), jnp.bfloat16)
    count = 3 if keep_kv else 1
    out_shapes = (out,) * count
    out_specs = (out_tile,) * count
    if query_rows is not None:
        assert not keep_kv and entry is None
        out_shapes = (jax.ShapeDtypeStruct((query_rows, width), jnp.bfloat16),)
        out_specs = (pl.BlockSpec((query_rows, block), lambda i, f: (0, i)),)
    if into is not None:
        assert query_rows is not None
        buffer, slot = into
        in_specs.append(pl.BlockSpec(memory_space=pl.ANY))
        operands.append(buffer)
        aliases = {len(operands): 0}
        out_shapes = (jax.ShapeDtypeStruct(buffer.shape, buffer.dtype),)
        out_specs = (pl.BlockSpec((None, query_rows, block), lambda i, f: (slot, 0, i)),)
    if emit_rows is not None:
        half, rows, slots = emit_rows
        out_shapes += (
            jax.ShapeDtypeStruct((half, width), jnp.bfloat16),
            jax.ShapeDtypeStruct((slots, rows, width), jnp.bfloat16),
        )
        out_specs += (
            pl.BlockSpec((half, block), lambda i, f: (0, i)),
            pl.BlockSpec((None, rows, block), lambda i, f: (0, 0, i)),
        )
    return pl.pallas_call(
        functools.partial(
            layer_kernel,
            two_sources=entry is not None,
            keep_kv=keep_kv,
            query_rows=query_rows,
            emit_rows=emit_rows is not None,
            aliased=into is not None,
            far_slabs=(far_k[1], far_v[1]),
        ),
        out_shape=out_shapes,
        grid_spec=pltpu.PrefetchScalarGridSpec(
            num_scalar_prefetch=1,
            grid=(width // block,),
            in_specs=in_specs,
            out_specs=out_specs,
            scratch_shapes=[
                pltpu.VMEM((tokens, width), jnp.bfloat16),
                pltpu.VMEM((tokens, width), jnp.bfloat16),
                pltpu.VMEM((query_rows or tokens, width), jnp.float32),
                pltpu.VMEM((query_rows or tokens, width), jnp.float32),
                pltpu.VMEM((query_rows or tokens, width), jnp.bfloat16),
                pltpu.SemaphoreType.DMA((2,)),
            ],
        ),
        input_output_aliases=aliases,
        cost_estimate=pl.CostEstimate(
            flops=8 * tokens * 2 * tokens * width,
            transcendentals=tokens * 2 * tokens * (width // HD),
            bytes_accessed=(4 + 2 * count) * tokens * width,
        ),
    )(flags, *operands)


def per_device(
    perturbed_frame_activation,
    inbound_activation,
    section_block_indices,
    tile_arrival_permutation,
    adaptive_shifting,
    adaptive_scaling,
    tier_query_factor,
    tier_skip_coefficient,
    earlier_step_lookup_matrix,
    earlier_step_content_matrix,
):
    segment = lax.axis_index("segment")
    place = lax.axis_index("ctx")
    patch_count = tile_arrival_permutation.shape[0]
    rows = inbound_activation.shape[1]
    width = inbound_activation.shape[2]
    slot_count = earlier_step_lookup_matrix.shape[1]
    layers_here = section_block_indices[0]

    def pick_patch(stack, patch, axis):
        chosen = lax.index_in_dim(stack, 0, axis, keepdims=False)
        for other in range(1, stack.shape[axis]):
            chosen = jnp.where(patch == other, lax.index_in_dim(stack, other, axis, keepdims=False), chosen)
        return chosen

    def arrival(position):
        chosen = tile_arrival_permutation[0]
        for index in range(1, patch_count):
            chosen = jnp.where(position == index, tile_arrival_permutation[index], chosen)
        return chosen

    first_rows = jnp.where(
        segment == 0,
        pick_patch(perturbed_frame_activation, tile_arrival_permutation[0], 0),
        inbound_activation[0],
    )
    entry_rows = [first_rows[None]]
    for turn in range(1, patch_count):
        entry_rows.append(pick_patch(perturbed_frame_activation, tile_arrival_permutation[turn], 0)[None])
    other_patch = arrival(jnp.mod(1 - segment, patch_count))
    far_k = pick_patch(earlier_step_lookup_matrix[0], other_patch, 1)
    far_v = pick_patch(earlier_step_content_matrix[0], other_patch, 1)
    packed = jnp.concatenate(entry_rows + [far_k, far_v], axis=0)
    whole = lax.all_gather(packed, "ctx", axis=1, tiled=True)
    params = [
        adaptive_shifting[0],
        adaptive_scaling[0],
        tier_query_factor[0],
        tier_skip_coefficient[0],
    ]
    first_segment = (segment == 0).astype(jnp.int32)
    core = jnp.mod(place, 2)
    half = rows * lax.axis_size("ctx") // 2

    def flags(tier):
        live = (layers_here > tier).astype(jnp.int32)
        return jnp.stack([live, first_segment, (place * rows).astype(jnp.int32), (core * half).astype(jnp.int32)])

    source = (whole, 0)
    turn_zero_kv = []
    for tier in range(slot_count):
        last = tier == slot_count - 1
        results = fused_layer(
            flags(tier),
            source,
            params,
            tier,
            (whole, patch_count + tier),
            (whole, patch_count + slot_count + tier),
            emit_rows=(half, rows, patch_count) if last else None,
        )
        state, fresh_key, fresh_value = results[:3]
        source = (state[None], 0)
        turn_zero_kv.append(((fresh_key[None], 0), (fresh_value[None], 0)))
    sent, outcomes = results[3:]
    count = lax.axis_size("segment")
    for turn in range(1, patch_count):
        got = lax.ppermute(sent, "segment", [(i, i + 1) for i in range(count - 1)])
        ctx_count = lax.axis_size("ctx")
        swapped = lax.ppermute(got, "ctx", [(c, c ^ 1) for c in range(ctx_count)])
        arrived = jnp.where(
            core == 0,
            jnp.concatenate([got, swapped], axis=0),
            jnp.concatenate([swapped, got], axis=0),
        )
        source = (arrived[None], 0)
        entry = (whole, turn)
        for tier in range(slot_count):
            last = tier == slot_count - 1
            if last:
                assert turn == patch_count - 1
                (outcomes,) = fused_layer(
                    flags(tier),
                    source,
                    params,
                    tier,
                    *turn_zero_kv[tier],
                    keep_kv=False,
                    query_rows=rows,
                    into=(outcomes, turn),
                )
            else:
                (state,) = fused_layer(
                    flags(tier), source, params, tier, *turn_zero_kv[tier], entry=entry, keep_kv=False
                )
                source = (state[None], 0)
                entry = None
    return outcomes[None]


def solution(mesh):
    return jax.shard_map(
        per_device,
        mesh=mesh,
        in_specs=(
            P(None, "ctx", None),
            P("segment", "ctx", None),
            P("segment"),
            P(),
            P("segment", None, None),
            P("segment", None, None),
            P("segment", None, None),
            P("segment", None, None),
            P("segment", None, None, "ctx", None),
            P("segment", None, None, "ctx", None),
        ),
        out_specs=P("segment", None, "ctx", None),
        check_vma=False,
    )
```

```python
import functools
import math

import jax
import jax.numpy as jnp
from jax import lax
from jax.experimental import pallas as pl
from jax.experimental.pallas import tpu as pltpu
from jax.sharding import PartitionSpec as P

HD = 128
EPSILON = 1e-06


def head_norm(values):
    return values * lax.rsqrt(jnp.mean(values * values, axis=-1, keepdims=True) + EPSILON)


def layer_kernel(flags_ref, *refs, two_sources, keep_kv, query_rows, emit_rows, aliased):
    if two_sources:
        full_ref, entry_full_ref, *refs = refs
        entry_x_ref = entry_full_ref
    else:
        full_ref, *refs = refs
    x_ref = full_ref
    shift_ref, stretch_ref, factor_ref, skip_ref, kf_ref, vf_ref, *refs = refs
    if aliased:
        refs = refs[1:]
    o_ref, *refs = refs
    kv_refs = refs[:2] if keep_kv else ()
    live = flags_ref[0] > 0
    scale = 1.0 / math.sqrt(HD)
    dims = (((1,), (1,)), ((), ()))
    whole = full_ref[...]
    state = x_ref[...]
    if two_sources:
        use_entry = flags_ref[1] > 0
        whole = jnp.where(use_entry, entry_full_ref[...], whole)
        state = jnp.where(use_entry, entry_x_ref[...], state)
    def row_scale_of(rows_value):
        rows_value = rows_value.astype(jnp.float32)
        return lax.rsqrt(jnp.mean(rows_value * rows_value, axis=-1, keepdims=True) + EPSILON)

    row_scale = row_scale_of(whole)
    if query_rows is None:
        state_q, row_scale_q = state, row_scale
    else:
        start = pl.multiple_of(flags_ref[2], query_rows)
        state_q = x_ref[pl.ds(start, query_rows), :]
        row_scale_q = row_scale_of(full_ref[pl.ds(start, query_rows), :])
    for j in range(state.shape[1] // HD):
        cols = slice(j * HD, (j + 1) * HD)
        stretch = 1.0 + stretch_ref[:, cols]
        x_all = state[:, cols].astype(jnp.float32)
        hidden = x_all * row_scale * stretch + shift_ref[:, cols]
        fresh_key = head_norm(hidden * factor_ref[:, cols]).astype(jnp.bfloat16)
        fresh_value = hidden.astype(jnp.bfloat16)
        x_rounded = state_q[:, cols]
        x = x_rounded.astype(jnp.float32)
        if query_rows is not None:
            hidden = x * row_scale_q * stretch + shift_ref[:, cols]
        query = head_norm(hidden).astype(jnp.bfloat16)
        if keep_kv:
            kv_refs[0][:, cols] = fresh_key
            kv_refs[1][:, cols] = fresh_value
        near = lax.dot_general(query, fresh_key, dims, preferred_element_type=jnp.float32) * scale
        far = lax.dot_general(query, kf_ref[:, cols], dims, preferred_element_type=jnp.float32) * scale
        near = jnp.exp(near)
        far = jnp.exp(far)
        total = jnp.sum(near, axis=-1, keepdims=True) + jnp.sum(far, axis=-1, keepdims=True)
        numerator = jnp.dot(
            near.astype(jnp.bfloat16), fresh_value, preferred_element_type=jnp.float32
        ) + jnp.dot(far.astype(jnp.bfloat16), vf_ref[:, cols], preferred_element_type=jnp.float32)
        attended = numerator / total
        new_state = (x + skip_ref[:, cols] * attended).astype(o_ref.dtype)
        o_ref[:, cols] = jnp.where(live, new_state, x_rounded)
    if emit_rows:
        half_ref, rows_ref = refs[len(kv_refs) :]
        half = half_ref.shape[0]
        rows = rows_ref.shape[0]
        half_ref[...] = o_ref[pl.ds(pl.multiple_of(flags_ref[3], half), half), :]
        rows_ref[...] = o_ref[pl.ds(pl.multiple_of(flags_ref[2], rows), rows), :]


def fused_layer(
    flags,
    source,
    params,
    tier,
    far_k,
    far_v,
    entry=None,
    keep_kv=True,
    query_rows=None,
    emit_rows=None,
    into=None,
):
    array, slab = source
    _, tokens, width = array.shape
    block = width

    def slab_specs(slab_index):
        return [pl.BlockSpec((None, tokens, width), lambda i, f: (slab_index, 0, 0))]

    def tile_of(slab_index):
        return pl.BlockSpec((None, tokens, block), lambda i, f: (slab_index, 0, i))

    line = pl.BlockSpec((None, 1, block), lambda i, f: (tier, 0, i))
    in_specs = slab_specs(slab)
    operands = [array]
    if entry is not None:
        in_specs += slab_specs(entry[1])
        operands += [entry[0]]
    in_specs += [line] * 4 + [tile_of(far_k[1]), tile_of(far_v[1])]
    operands += [p.reshape(p.shape[0], 1, width) for p in params] + [far_k[0], far_v[0]]
    aliases = {}
    out_tile = pl.BlockSpec((tokens, block), lambda i, f: (0, i))
    out = jax.ShapeDtypeStruct((tokens, width), jnp.bfloat16)
    count = 3 if keep_kv else 1
    out_shapes = (out,) * count
    out_specs = (out_tile,) * count
    if query_rows is not None:
        assert not keep_kv and entry is None
        out_shapes = (jax.ShapeDtypeStruct((query_rows, width), jnp.bfloat16),)
        out_specs = (pl.BlockSpec((query_rows, block), lambda i, f: (0, i)),)
    if into is not None:
        assert query_rows is not None
        buffer, slot = into
        in_specs.append(pl.BlockSpec(memory_space=pl.ANY))
        operands.append(buffer)
        aliases = {len(operands): 0}
        out_shapes = (jax.ShapeDtypeStruct(buffer.shape, buffer.dtype),)
        out_specs = (pl.BlockSpec((None, query_rows, block), lambda i, f: (slot, 0, i)),)
    if emit_rows is not None:
        half, rows, slots = emit_rows
        out_shapes += (
            jax.ShapeDtypeStruct((half, width), jnp.bfloat16),
            jax.ShapeDtypeStruct((slots, rows, width), jnp.bfloat16),
        )
        out_specs += (
            pl.BlockSpec((half, block), lambda i, f: (0, i)),
            pl.BlockSpec((None, rows, block), lambda i, f: (0, 0, i)),
        )
    return pl.pallas_call(
        functools.partial(
            layer_kernel,
            two_sources=entry is not None,
            keep_kv=keep_kv,
            query_rows=query_rows,
            emit_rows=emit_rows is not None,
            aliased=into is not None,
        ),
        out_shape=out_shapes,
        grid_spec=pltpu.PrefetchScalarGridSpec(
            num_scalar_prefetch=1,
            grid=(width // block,),
            in_specs=in_specs,
            out_specs=out_specs,
        ),
        input_output_aliases=aliases,
        cost_estimate=pl.CostEstimate(
            flops=8 * tokens * 2 * tokens * width,
            transcendentals=tokens * 2 * tokens * (width // HD),
            bytes_accessed=(4 + 2 * count) * tokens * width,
        ),
    )(flags, *operands)


def per_device(
    perturbed_frame_activation,
    inbound_activation,
    section_block_indices,
    tile_arrival_permutation,
    adaptive_shifting,
    adaptive_scaling,
    tier_query_factor,
    tier_skip_coefficient,
    earlier_step_lookup_matrix,
    earlier_step_content_matrix,
):
    segment = lax.axis_index("segment")
    place = lax.axis_index("ctx")
    patch_count = tile_arrival_permutation.shape[0]
    rows = inbound_activation.shape[1]
    width = inbound_activation.shape[2]
    slot_count = earlier_step_lookup_matrix.shape[1]
    layers_here = section_block_indices[0]

    def pick_patch(stack, patch, axis):
        chosen = lax.index_in_dim(stack, 0, axis, keepdims=False)
        for other in range(1, stack.shape[axis]):
            chosen = jnp.where(patch == other, lax.index_in_dim(stack, other, axis, keepdims=False), chosen)
        return chosen

    def arrival(position):
        chosen = tile_arrival_permutation[0]
        for index in range(1, patch_count):
            chosen = jnp.where(position == index, tile_arrival_permutation[index], chosen)
        return chosen

    first_rows = jnp.where(
        segment == 0,
        pick_patch(perturbed_frame_activation, tile_arrival_permutation[0], 0),
        inbound_activation[0],
    )
    entry_rows = [first_rows[None]]
    for turn in range(1, patch_count):
        entry_rows.append(pick_patch(perturbed_frame_activation, tile_arrival_permutation[turn], 0)[None])
    other_patch = arrival(jnp.mod(1 - segment, patch_count))
    candidates = [
        jnp.concatenate(
            entry_rows
            + [earlier_step_lookup_matrix[0, :, patch], earlier_step_content_matrix[0, :, patch]],
            axis=0,
        )
        for patch in range(patch_count)
    ]
    packed = candidates[0]
    for patch in range(1, patch_count):
        packed = jnp.where(other_patch == patch, candidates[patch], packed)
    whole = lax.all_gather(packed, "ctx", axis=1, tiled=True)
    params = [
        adaptive_shifting[0],
        adaptive_scaling[0],
        tier_query_factor[0],
        tier_skip_coefficient[0],
    ]
    first_segment = (segment == 0).astype(jnp.int32)
    core = jnp.mod(place, 2)
    half = rows * lax.axis_size("ctx") // 2

    def flags(tier):
        live = (layers_here > tier).astype(jnp.int32)
        return jnp.stack([live, first_segment, (place * rows).astype(jnp.int32), (core * half).astype(jnp.int32)])

    source = (whole, 0)
    turn_zero_kv = []
    for tier in range(slot_count):
        last = tier == slot_count - 1
        results = fused_layer(
            flags(tier),
            source,
            params,
            tier,
            (whole, patch_count + tier),
            (whole, patch_count + slot_count + tier),
            emit_rows=(half, rows, patch_count) if last else None,
        )
        state, fresh_key, fresh_value = results[:3]
        source = (state[None], 0)
        turn_zero_kv.append(((fresh_key[None], 0), (fresh_value[None], 0)))
    sent, outcomes = results[3:]
    count = lax.axis_size("segment")
    for turn in range(1, patch_count):
        got = lax.ppermute(sent, "segment", [(i, i + 1) for i in range(count - 1)])
        ctx_count = lax.axis_size("ctx")
        swapped = lax.ppermute(got, "ctx", [(c, c ^ 1) for c in range(ctx_count)])
        arrived = jnp.where(
            core == 0,
            jnp.concatenate([got, swapped], axis=0),
            jnp.concatenate([swapped, got], axis=0),
        )
        source = (arrived[None], 0)
        entry = (whole, turn)
        for tier in range(slot_count):
            last = tier == slot_count - 1
            if last:
                assert turn == patch_count - 1
                (outcomes,) = fused_layer(
                    flags(tier),
                    source,
                    params,
                    tier,
                    *turn_zero_kv[tier],
                    keep_kv=False,
                    query_rows=rows,
                    into=(outcomes, turn),
                )
            else:
                (state,) = fused_layer(
                    flags(tier), source, params, tier, *turn_zero_kv[tier], entry=entry, keep_kv=False
                )
                source = (state[None], 0)
                entry = None
    return outcomes[None]


def solution(mesh):
    return jax.shard_map(
        per_device,
        mesh=mesh,
        in_specs=(
            P(None, "ctx", None),
            P("segment", "ctx", None),
            P("segment"),
            P(),
            P("segment", None, None),
            P("segment", None, None),
            P("segment", None, None),
            P("segment", None, None),
            P("segment", None, None, "ctx", None),
            P("segment", None, None, "ctx", None),
        ),
        out_specs=P("segment", None, "ctx", None),
        check_vma=False,
    )
```

```python
import functools
import math

import jax
import jax.numpy as jnp
from jax import lax
from jax.experimental import pallas as pl
from jax.experimental.pallas import tpu as pltpu
from jax.sharding import PartitionSpec as P

HD = 128
EPSILON = 1e-06


def head_norm(values):
    return values * lax.rsqrt(jnp.mean(values * values, axis=-1, keepdims=True) + EPSILON)


def layer_kernel(flags_ref, *refs, two_sources, keep_kv, query_rows, emit_rows, aliased, halves):
    if halves:
        received_ref, partner_ref, *refs = refs
        received_first = flags_ref[3] == 0
        received, partner = received_ref[...], partner_ref[...]
        arrived = jnp.concatenate(
            [jnp.where(received_first, received, partner), jnp.where(received_first, partner, received)],
            axis=0,
        )
    else:
        full_ref, *refs = refs
        x_ref = full_ref
    if two_sources:
        entry_full_ref, *refs = refs
        entry_x_ref = entry_full_ref
    shift_ref, stretch_ref, factor_ref, skip_ref, kf_ref, vf_ref, *refs = refs
    if aliased:
        refs = refs[1:]
    o_ref, *refs = refs
    kv_refs = refs[:2] if keep_kv else ()
    live = flags_ref[0] > 0
    scale = 1.0 / math.sqrt(HD)
    dims = (((1,), (1,)), ((), ()))
    if halves:
        assert query_rows is None
        whole = state = arrived
    else:
        whole = full_ref[...]
        state = x_ref[...]
    if two_sources:
        use_entry = flags_ref[1] > 0
        whole = jnp.where(use_entry, entry_full_ref[...], whole)
        state = jnp.where(use_entry, entry_x_ref[...], state)
    def row_scale_of(rows_value):
        rows_value = rows_value.astype(jnp.float32)
        return lax.rsqrt(jnp.mean(rows_value * rows_value, axis=-1, keepdims=True) + EPSILON)

    row_scale = row_scale_of(whole)
    if query_rows is None:
        state_q, row_scale_q = state, row_scale
    else:
        start = pl.multiple_of(flags_ref[2], query_rows)
        state_q = x_ref[pl.ds(start, query_rows), :]
        row_scale_q = row_scale_of(full_ref[pl.ds(start, query_rows), :])
    for j in range(state.shape[1] // HD):
        cols = slice(j * HD, (j + 1) * HD)
        stretch = 1.0 + stretch_ref[:, cols]
        x_all = state[:, cols].astype(jnp.float32)
        hidden = x_all * row_scale * stretch + shift_ref[:, cols]
        fresh_key = head_norm(hidden * factor_ref[:, cols]).astype(jnp.bfloat16)
        fresh_value = hidden.astype(jnp.bfloat16)
        x_rounded = state_q[:, cols]
        x = x_rounded.astype(jnp.float32)
        if query_rows is not None:
            hidden = x * row_scale_q * stretch + shift_ref[:, cols]
        query = head_norm(hidden).astype(jnp.bfloat16)
        if keep_kv:
            kv_refs[0][:, cols] = fresh_key
            kv_refs[1][:, cols] = fresh_value
        near = lax.dot_general(query, fresh_key, dims, preferred_element_type=jnp.float32) * scale
        far = lax.dot_general(query, kf_ref[:, cols], dims, preferred_element_type=jnp.float32) * scale
        near = jnp.exp(near)
        far = jnp.exp(far)
        total = jnp.sum(near, axis=-1, keepdims=True) + jnp.sum(far, axis=-1, keepdims=True)
        numerator = jnp.dot(
            near.astype(jnp.bfloat16), fresh_value, preferred_element_type=jnp.float32
        ) + jnp.dot(far.astype(jnp.bfloat16), vf_ref[:, cols], preferred_element_type=jnp.float32)
        attended = numerator / total
        new_state = (x + skip_ref[:, cols] * attended).astype(o_ref.dtype)
        o_ref[:, cols] = jnp.where(live, new_state, x_rounded)
    if emit_rows:
        half_ref, rows_ref = refs[len(kv_refs) :]
        half = half_ref.shape[0]
        rows = rows_ref.shape[0]
        half_ref[...] = o_ref[pl.ds(pl.multiple_of(flags_ref[3], half), half), :]
        rows_ref[...] = o_ref[pl.ds(pl.multiple_of(flags_ref[2], rows), rows), :]


def fused_layer(
    flags,
    source,
    params,
    tier,
    far_k,
    far_v,
    entry=None,
    keep_kv=True,
    query_rows=None,
    emit_rows=None,
    into=None,
):
    halves = isinstance(source, list)
    if halves:
        tokens = source[0].shape[0] * 2
        width = source[0].shape[1]
    else:
        array, slab = source
        _, tokens, width = array.shape
    block = width

    def slab_specs(slab_index):
        return [pl.BlockSpec((None, tokens, width), lambda i, f: (slab_index, 0, 0))]

    def tile_of(slab_index):
        return pl.BlockSpec((None, tokens, block), lambda i, f: (slab_index, 0, i))

    line = pl.BlockSpec((None, 1, block), lambda i, f: (tier, 0, i))
    if halves:
        in_specs = [pl.BlockSpec((tokens // 2, width), lambda i, f: (0, 0))] * 2
        operands = list(source)
    else:
        in_specs = slab_specs(slab)
        operands = [array]
    if entry is not None:
        in_specs += slab_specs(entry[1])
        operands += [entry[0]]
    in_specs += [line] * 4 + [tile_of(far_k[1]), tile_of(far_v[1])]
    operands += [p.reshape(p.shape[0], 1, width) for p in params] + [far_k[0], far_v[0]]
    aliases = {}
    out_tile = pl.BlockSpec((tokens, block), lambda i, f: (0, i))
    out = jax.ShapeDtypeStruct((tokens, width), jnp.bfloat16)
    count = 3 if keep_kv else 1
    out_shapes = (out,) * count
    out_specs = (out_tile,) * count
    if query_rows is not None:
        assert not keep_kv and entry is None
        out_shapes = (jax.ShapeDtypeStruct((query_rows, width), jnp.bfloat16),)
        out_specs = (pl.BlockSpec((query_rows, block), lambda i, f: (0, i)),)
    if into is not None:
        assert query_rows is not None
        buffer, slot = into
        in_specs.append(pl.BlockSpec(memory_space=pl.ANY))
        operands.append(buffer)
        aliases = {len(operands): 0}
        out_shapes = (jax.ShapeDtypeStruct(buffer.shape, buffer.dtype),)
        out_specs = (pl.BlockSpec((None, query_rows, block), lambda i, f: (slot, 0, i)),)
    if emit_rows is not None:
        half, rows, slots = emit_rows
        out_shapes += (
            jax.ShapeDtypeStruct((half, width), jnp.bfloat16),
            jax.ShapeDtypeStruct((slots, rows, width), jnp.bfloat16),
        )
        out_specs += (
            pl.BlockSpec((half, block), lambda i, f: (0, i)),
            pl.BlockSpec((None, rows, block), lambda i, f: (0, 0, i)),
        )
    return pl.pallas_call(
        functools.partial(
            layer_kernel,
            two_sources=entry is not None,
            keep_kv=keep_kv,
            query_rows=query_rows,
            emit_rows=emit_rows is not None,
            aliased=into is not None,
            halves=halves,
        ),
        out_shape=out_shapes,
        grid_spec=pltpu.PrefetchScalarGridSpec(
            num_scalar_prefetch=1,
            grid=(width // block,),
            in_specs=in_specs,
            out_specs=out_specs,
        ),
        input_output_aliases=aliases,
        cost_estimate=pl.CostEstimate(
            flops=8 * tokens * 2 * tokens * width,
            transcendentals=tokens * 2 * tokens * (width // HD),
            bytes_accessed=(4 + 2 * count) * tokens * width,
        ),
    )(flags, *operands)


def per_device(
    perturbed_frame_activation,
    inbound_activation,
    section_block_indices,
    tile_arrival_permutation,
    adaptive_shifting,
    adaptive_scaling,
    tier_query_factor,
    tier_skip_coefficient,
    earlier_step_lookup_matrix,
    earlier_step_content_matrix,
):
    segment = lax.axis_index("segment")
    place = lax.axis_index("ctx")
    patch_count = tile_arrival_permutation.shape[0]
    rows = inbound_activation.shape[1]
    width = inbound_activation.shape[2]
    slot_count = earlier_step_lookup_matrix.shape[1]
    layers_here = section_block_indices[0]

    def pick_patch(stack, patch, axis):
        chosen = lax.index_in_dim(stack, 0, axis, keepdims=False)
        for other in range(1, stack.shape[axis]):
            chosen = jnp.where(patch == other, lax.index_in_dim(stack, other, axis, keepdims=False), chosen)
        return chosen

    def arrival(position):
        chosen = tile_arrival_permutation[0]
        for index in range(1, patch_count):
            chosen = jnp.where(position == index, tile_arrival_permutation[index], chosen)
        return chosen

    first_rows = jnp.where(
        segment == 0,
        pick_patch(perturbed_frame_activation, tile_arrival_permutation[0], 0),
        inbound_activation[0],
    )
    entry_rows = [first_rows[None]]
    for turn in range(1, patch_count):
        entry_rows.append(pick_patch(perturbed_frame_activation, tile_arrival_permutation[turn], 0)[None])
    other_patch = arrival(jnp.mod(1 - segment, patch_count))
    candidates = [
        jnp.concatenate(
            entry_rows
            + [earlier_step_lookup_matrix[0, :, patch], earlier_step_content_matrix[0, :, patch]],
            axis=0,
        )
        for patch in range(patch_count)
    ]
    packed = candidates[0]
    for patch in range(1, patch_count):
        packed = jnp.where(other_patch == patch, candidates[patch], packed)
    whole = lax.all_gather(packed, "ctx", axis=1, tiled=True)
    params = [
        adaptive_shifting[0],
        adaptive_scaling[0],
        tier_query_factor[0],
        tier_skip_coefficient[0],
    ]
    first_segment = (segment == 0).astype(jnp.int32)
    core = jnp.mod(place, 2)
    half = rows * lax.axis_size("ctx") // 2

    def flags(tier):
        live = (layers_here > tier).astype(jnp.int32)
        return jnp.stack([live, first_segment, (place * rows).astype(jnp.int32), (core * half).astype(jnp.int32)])

    source = (whole, 0)
    turn_zero_kv = []
    for tier in range(slot_count):
        last = tier == slot_count - 1
        results = fused_layer(
            flags(tier),
            source,
            params,
            tier,
            (whole, patch_count + tier),
            (whole, patch_count + slot_count + tier),
            emit_rows=(half, rows, patch_count) if last else None,
        )
        state, fresh_key, fresh_value = results[:3]
        source = (state[None], 0)
        turn_zero_kv.append(((fresh_key[None], 0), (fresh_value[None], 0)))
    sent, outcomes = results[3:]
    count = lax.axis_size("segment")
    for turn in range(1, patch_count):
        got = lax.ppermute(sent, "segment", [(i, i + 1) for i in range(count - 1)])
        ctx_count = lax.axis_size("ctx")
        swapped = lax.ppermute(got, "ctx", [(c, c ^ 1) for c in range(ctx_count)])
        source = [got, swapped]
        entry = (whole, turn)
        for tier in range(slot_count):
            last = tier == slot_count - 1
            if last:
                assert turn == patch_count - 1
                (outcomes,) = fused_layer(
                    flags(tier),
                    source,
                    params,
                    tier,
                    *turn_zero_kv[tier],
                    keep_kv=False,
                    query_rows=rows,
                    into=(outcomes, turn),
                )
            else:
                (state,) = fused_layer(
                    flags(tier), source, params, tier, *turn_zero_kv[tier], entry=entry, keep_kv=False
                )
                source = (state[None], 0)
                entry = None
    return outcomes[None]


def solution(mesh):
    return jax.shard_map(
        per_device,
        mesh=mesh,
        in_specs=(
            P(None, "ctx", None),
            P("segment", "ctx", None),
            P("segment"),
            P(),
            P("segment", None, None),
            P("segment", None, None),
            P("segment", None, None),
            P("segment", None, None),
            P("segment", None, None, "ctx", None),
            P("segment", None, None, "ctx", None),
        ),
        out_specs=P("segment", None, "ctx", None),
        check_vma=False,
    )
```

```python
import functools
import math

import jax
import jax.numpy as jnp
from jax import lax
from jax.experimental import pallas as pl
from jax.experimental.pallas import tpu as pltpu
from jax.sharding import PartitionSpec as P

HD = 128
EPSILON = 1e-06


def head_norm(values):
    return values * lax.rsqrt(jnp.mean(values * values, axis=-1, keepdims=True) + EPSILON)


def layer_kernel(flags_ref, *refs, two_sources, keep_kv, query_rows, emit_rows, aliased, halves):
    if halves:
        received_ref, partner_ref, *refs = refs
        received_first = flags_ref[3] == 0
        received, partner = received_ref[...], partner_ref[...]
        arrived = jnp.concatenate(
            [jnp.where(received_first, received, partner), jnp.where(received_first, partner, received)],
            axis=0,
        )
    else:
        full_ref, *refs = refs
        x_ref = full_ref
    if two_sources:
        entry_full_ref, *refs = refs
        entry_x_ref = entry_full_ref
    shift_ref, stretch_ref, factor_ref, skip_ref, kf_ref, vf_ref, *refs = refs
    if aliased:
        refs = refs[1:]
    if emit_rows:
        k_ref, v_ref, half_ref, rows_ref = refs
        kv_refs = (k_ref, v_ref)
        query_sets = [(flags_ref[3], half_ref), (flags_ref[2], rows_ref)]
    else:
        o_ref, *refs = refs
        kv_refs = refs[:2] if keep_kv else ()
        query_sets = [(None if query_rows is None else flags_ref[2], o_ref)]
    live = flags_ref[0] > 0
    scale = 1.0 / math.sqrt(HD)
    dims = (((1,), (1,)), ((), ()))
    if halves:
        assert query_rows is None
        whole = state = arrived
    else:
        whole = full_ref[...]
        state = x_ref[...]
    if two_sources:
        use_entry = flags_ref[1] > 0
        whole = jnp.where(use_entry, entry_full_ref[...], whole)
        state = jnp.where(use_entry, entry_x_ref[...], state)

    def row_scale_of(rows_value):
        rows_value = rows_value.astype(jnp.float32)
        return lax.rsqrt(jnp.mean(rows_value * rows_value, axis=-1, keepdims=True) + EPSILON)

    row_scale = row_scale_of(whole)
    picked = []
    for start, out_ref in query_sets:
        if start is None:
            picked.append((state, row_scale, out_ref, False))
        else:
            count = out_ref.shape[0]
            start = pl.multiple_of(start, count)
            picked.append(
                (
                    x_ref[pl.ds(start, count), :],
                    row_scale_of(full_ref[pl.ds(start, count), :]),
                    out_ref,
                    True,
                )
            )
    for j in range(state.shape[1] // HD):
        cols = slice(j * HD, (j + 1) * HD)
        stretch = 1.0 + stretch_ref[:, cols]
        x_all = state[:, cols].astype(jnp.float32)
        hidden_all = x_all * row_scale * stretch + shift_ref[:, cols]
        fresh_key = head_norm(hidden_all * factor_ref[:, cols]).astype(jnp.bfloat16)
        fresh_value = hidden_all.astype(jnp.bfloat16)
        if kv_refs:
            kv_refs[0][:, cols] = fresh_key
            kv_refs[1][:, cols] = fresh_value
        for state_q, row_scale_q, out_ref, separate in picked:
            x_rounded = state_q[:, cols]
            x = x_rounded.astype(jnp.float32)
            hidden = x * row_scale_q * stretch + shift_ref[:, cols] if separate else hidden_all
            query = head_norm(hidden).astype(jnp.bfloat16)
            near = lax.dot_general(query, fresh_key, dims, preferred_element_type=jnp.float32) * scale
            far = lax.dot_general(query, kf_ref[:, cols], dims, preferred_element_type=jnp.float32) * scale
            near = jnp.exp(near)
            far = jnp.exp(far)
            total = jnp.sum(near, axis=-1, keepdims=True) + jnp.sum(far, axis=-1, keepdims=True)
            numerator = jnp.dot(
                near.astype(jnp.bfloat16), fresh_value, preferred_element_type=jnp.float32
            ) + jnp.dot(far.astype(jnp.bfloat16), vf_ref[:, cols], preferred_element_type=jnp.float32)
            attended = numerator / total
            new_state = (x + skip_ref[:, cols] * attended).astype(out_ref.dtype)
            out_ref[:, cols] = jnp.where(live, new_state, x_rounded)


def fused_layer(
    flags,
    source,
    params,
    tier,
    far_k,
    far_v,
    entry=None,
    keep_kv=True,
    query_rows=None,
    emit_rows=None,
    into=None,
):
    halves = isinstance(source, list)
    if halves:
        tokens = source[0].shape[0] * 2
        width = source[0].shape[1]
    else:
        array, slab = source
        _, tokens, width = array.shape
    block = width

    def slab_specs(slab_index):
        return [pl.BlockSpec((None, tokens, width), lambda i, f: (slab_index, 0, 0))]

    def tile_of(slab_index):
        return pl.BlockSpec((None, tokens, block), lambda i, f: (slab_index, 0, i))

    line = pl.BlockSpec((None, 1, block), lambda i, f: (tier, 0, i))
    if halves:
        in_specs = [pl.BlockSpec((tokens // 2, width), lambda i, f: (0, 0))] * 2
        operands = list(source)
    else:
        in_specs = slab_specs(slab)
        operands = [array]
    if entry is not None:
        in_specs += slab_specs(entry[1])
        operands += [entry[0]]
    in_specs += [line] * 4 + [tile_of(far_k[1]), tile_of(far_v[1])]
    operands += [p.reshape(p.shape[0], 1, width) for p in params] + [far_k[0], far_v[0]]
    aliases = {}
    out_tile = pl.BlockSpec((tokens, block), lambda i, f: (0, i))
    out = jax.ShapeDtypeStruct((tokens, width), jnp.bfloat16)
    count = 3 if keep_kv else 1
    out_shapes = (out,) * count
    out_specs = (out_tile,) * count
    if query_rows is not None:
        assert not keep_kv and entry is None
        out_shapes = (jax.ShapeDtypeStruct((query_rows, width), jnp.bfloat16),)
        out_specs = (pl.BlockSpec((query_rows, block), lambda i, f: (0, i)),)
    if into is not None:
        assert query_rows is not None
        buffer, slot = into
        in_specs.append(pl.BlockSpec(memory_space=pl.ANY))
        operands.append(buffer)
        aliases = {len(operands): 0}
        out_shapes = (jax.ShapeDtypeStruct(buffer.shape, buffer.dtype),)
        out_specs = (pl.BlockSpec((None, query_rows, block), lambda i, f: (slot, 0, i)),)
    if emit_rows is not None:
        assert keep_kv and entry is None and query_rows is None and not halves
        half, rows, slots = emit_rows
        out_shapes, out_specs = out_shapes[1:], out_specs[1:]
        out_shapes += (
            jax.ShapeDtypeStruct((half, width), jnp.bfloat16),
            jax.ShapeDtypeStruct((slots, rows, width), jnp.bfloat16),
        )
        out_specs += (
            pl.BlockSpec((half, block), lambda i, f: (0, i)),
            pl.BlockSpec((None, rows, block), lambda i, f: (0, 0, i)),
        )
    return pl.pallas_call(
        functools.partial(
            layer_kernel,
            two_sources=entry is not None,
            keep_kv=keep_kv,
            query_rows=query_rows,
            emit_rows=emit_rows is not None,
            aliased=into is not None,
            halves=halves,
        ),
        out_shape=out_shapes,
        grid_spec=pltpu.PrefetchScalarGridSpec(
            num_scalar_prefetch=1,
            grid=(width // block,),
            in_specs=in_specs,
            out_specs=out_specs,
        ),
        input_output_aliases=aliases,
        cost_estimate=pl.CostEstimate(
            flops=8 * tokens * 2 * tokens * width,
            transcendentals=tokens * 2 * tokens * (width // HD),
            bytes_accessed=(4 + 2 * count) * tokens * width,
        ),
    )(flags, *operands)


def per_device(
    perturbed_frame_activation,
    inbound_activation,
    section_block_indices,
    tile_arrival_permutation,
    adaptive_shifting,
    adaptive_scaling,
    tier_query_factor,
    tier_skip_coefficient,
    earlier_step_lookup_matrix,
    earlier_step_content_matrix,
):
    segment = lax.axis_index("segment")
    place = lax.axis_index("ctx")
    patch_count = tile_arrival_permutation.shape[0]
    rows = inbound_activation.shape[1]
    width = inbound_activation.shape[2]
    slot_count = earlier_step_lookup_matrix.shape[1]
    layers_here = section_block_indices[0]

    def pick_patch(stack, patch, axis):
        chosen = lax.index_in_dim(stack, 0, axis, keepdims=False)
        for other in range(1, stack.shape[axis]):
            chosen = jnp.where(patch == other, lax.index_in_dim(stack, other, axis, keepdims=False), chosen)
        return chosen

    def arrival(position):
        chosen = tile_arrival_permutation[0]
        for index in range(1, patch_count):
            chosen = jnp.where(position == index, tile_arrival_permutation[index], chosen)
        return chosen

    first_rows = jnp.where(
        segment == 0,
        pick_patch(perturbed_frame_activation, tile_arrival_permutation[0], 0),
        inbound_activation[0],
    )
    entry_rows = [first_rows[None]]
    for turn in range(1, patch_count):
        entry_rows.append(pick_patch(perturbed_frame_activation, tile_arrival_permutation[turn], 0)[None])
    other_patch = arrival(jnp.mod(1 - segment, patch_count))
    candidates = [
        jnp.concatenate(
            entry_rows
            + [earlier_step_lookup_matrix[0, :, patch], earlier_step_content_matrix[0, :, patch]],
            axis=0,
        )
        for patch in range(patch_count)
    ]
    packed = candidates[0]
    for patch in range(1, patch_count):
        packed = jnp.where(other_patch == patch, candidates[patch], packed)
    whole = lax.all_gather(packed, "ctx", axis=1, tiled=True)
    params = [
        adaptive_shifting[0],
        adaptive_scaling[0],
        tier_query_factor[0],
        tier_skip_coefficient[0],
    ]
    first_segment = (segment == 0).astype(jnp.int32)
    core = jnp.mod(place, 2)
    half = rows * lax.axis_size("ctx") // 2

    def flags(tier):
        live = (layers_here > tier).astype(jnp.int32)
        return jnp.stack([live, first_segment, (place * rows).astype(jnp.int32), (core * half).astype(jnp.int32)])

    source = (whole, 0)
    turn_zero_kv = []
    for tier in range(slot_count):
        last = tier == slot_count - 1
        results = fused_layer(
            flags(tier),
            source,
            params,
            tier,
            (whole, patch_count + tier),
            (whole, patch_count + slot_count + tier),
            emit_rows=(half, rows, patch_count) if last else None,
        )
        if last:
            fresh_key, fresh_value, sent, outcomes = results
        else:
            state, fresh_key, fresh_value = results
            source = (state[None], 0)
        turn_zero_kv.append(((fresh_key[None], 0), (fresh_value[None], 0)))
    count = lax.axis_size("segment")
    for turn in range(1, patch_count):
        got = lax.ppermute(sent, "segment", [(i, i + 1) for i in range(count - 1)])
        ctx_count = lax.axis_size("ctx")
        swapped = lax.ppermute(got, "ctx", [(c, c ^ 1) for c in range(ctx_count)])
        source = [got, swapped]
        entry = (whole, turn)
        for tier in range(slot_count):
            last = tier == slot_count - 1
            if last:
                assert turn == patch_count - 1
                (outcomes,) = fused_layer(
                    flags(tier),
                    source,
                    params,
                    tier,
                    *turn_zero_kv[tier],
                    keep_kv=False,
                    query_rows=rows,
                    into=(outcomes, turn),
                )
            else:
                (state,) = fused_layer(
                    flags(tier), source, params, tier, *turn_zero_kv[tier], entry=entry, keep_kv=False
                )
                source = (state[None], 0)
                entry = None
    return outcomes[None]


def solution(mesh):
    return jax.shard_map(
        per_device,
        mesh=mesh,
        in_specs=(
            P(None, "ctx", None),
            P("segment", "ctx", None),
            P("segment"),
            P(),
            P("segment", None, None),
            P("segment", None, None),
            P("segment", None, None),
            P("segment", None, None),
            P("segment", None, None, "ctx", None),
            P("segment", None, None, "ctx", None),
        ),
        out_specs=P("segment", None, "ctx", None),
        check_vma=False,
    )
```

```python
import functools
import math

import jax
import jax.numpy as jnp
from jax import lax
from jax.experimental import pallas as pl
from jax.experimental.pallas import tpu as pltpu
from jax.sharding import PartitionSpec as P

HD = 128
EPSILON = 1e-06


def head_norm(values):
    return values * lax.rsqrt(jnp.mean(values * values, axis=-1, keepdims=True) + EPSILON)


def layer_kernel(flags_ref, *refs, two_sources, keep_kv, query_rows, emit_rows, aliased, halves):
    if halves:
        received_ref, partner_ref, *refs = refs
        received_first = flags_ref[3] == 0
        received, partner = received_ref[...], partner_ref[...]
        arrived = jnp.concatenate(
            [jnp.where(received_first, received, partner), jnp.where(received_first, partner, received)],
            axis=0,
        )
    else:
        full_ref, *refs = refs
        x_ref = full_ref
    if two_sources:
        entry_full_ref, *refs = refs
        entry_x_ref = entry_full_ref
    shift_ref, stretch_ref, factor_ref, skip_ref, kf_ref, vf_ref, *refs = refs
    if aliased:
        refs = refs[1:]
    o_ref, *refs = refs
    kv_refs = refs[:2] if keep_kv else ()
    live = flags_ref[0] > 0
    scale = 1.0 / math.sqrt(HD)
    dims = (((1,), (1,)), ((), ()))
    if halves:
        assert query_rows is None
        whole = state = arrived
    else:
        whole = full_ref[...]
        state = x_ref[...]
    if two_sources:
        use_entry = flags_ref[1] > 0
        whole = jnp.where(use_entry, entry_full_ref[...], whole)
        state = jnp.where(use_entry, entry_x_ref[...], state)
    def row_scale_of(rows_value):
        rows_value = rows_value.astype(jnp.float32)
        return lax.rsqrt(jnp.mean(rows_value * rows_value, axis=-1, keepdims=True) + EPSILON)

    row_scale = row_scale_of(whole)
    if query_rows is None:
        state_q, row_scale_q = state, row_scale
    else:
        start = pl.multiple_of(flags_ref[2], query_rows)
        state_q = x_ref[pl.ds(start, query_rows), :]
        row_scale_q = row_scale_of(full_ref[pl.ds(start, query_rows), :])
    for j in range(state.shape[1] // HD):
        cols = slice(j * HD, (j + 1) * HD)
        stretch = 1.0 + stretch_ref[:, cols]
        x_all = state[:, cols].astype(jnp.float32)
        hidden = x_all * row_scale * stretch + shift_ref[:, cols]
        fresh_key = head_norm(hidden * factor_ref[:, cols]).astype(jnp.bfloat16)
        fresh_value = hidden.astype(jnp.bfloat16)
        x_rounded = state_q[:, cols]
        x = x_rounded.astype(jnp.float32)
        if query_rows is not None:
            hidden = x * row_scale_q * stretch + shift_ref[:, cols]
        query = head_norm(hidden).astype(jnp.bfloat16)
        if keep_kv:
            kv_refs[0][:, cols] = fresh_key
            kv_refs[1][:, cols] = fresh_value
        near = lax.dot_general(query, fresh_key, dims, preferred_element_type=jnp.float32) * scale
        far = lax.dot_general(query, kf_ref[:, cols], dims, preferred_element_type=jnp.float32) * scale
        near = jnp.exp(near)
        far = jnp.exp(far)
        total = jnp.sum(near, axis=-1, keepdims=True) + jnp.sum(far, axis=-1, keepdims=True)
        numerator = jnp.dot(
            near.astype(jnp.bfloat16), fresh_value, preferred_element_type=jnp.float32
        ) + jnp.dot(far.astype(jnp.bfloat16), vf_ref[:, cols], preferred_element_type=jnp.float32)
        attended = numerator / total
        new_state = (x + skip_ref[:, cols] * attended).astype(o_ref.dtype)
        o_ref[:, cols] = jnp.where(live, new_state, x_rounded)
    if emit_rows:
        half_ref, rows_ref = refs[len(kv_refs) :]
        half = half_ref.shape[0]
        rows = rows_ref.shape[0]
        half_ref[...] = o_ref[pl.ds(pl.multiple_of(flags_ref[3], half), half), :]
        rows_ref[...] = o_ref[pl.ds(pl.multiple_of(flags_ref[2], rows), rows), :]


def fused_layer(
    flags,
    source,
    params,
    tier,
    far_k,
    far_v,
    entry=None,
    keep_kv=True,
    query_rows=None,
    emit_rows=None,
    into=None,
):
    halves = isinstance(source, list)
    if halves:
        tokens = source[0].shape[0] * 2
        width = source[0].shape[1]
    else:
        array, slab = source
        _, tokens, width = array.shape
    block = width

    def slab_specs(slab_index):
        return [pl.BlockSpec((None, tokens, width), lambda i, f: (slab_index, 0, 0))]

    def tile_of(slab_index):
        return pl.BlockSpec((None, tokens, block), lambda i, f: (slab_index, 0, i))

    line = pl.BlockSpec((None, 1, block), lambda i, f: (tier, 0, i))
    if halves:
        in_specs = [pl.BlockSpec((tokens // 2, width), lambda i, f: (0, 0))] * 2
        operands = list(source)
    else:
        in_specs = slab_specs(slab)
        operands = [array]
    if entry is not None:
        in_specs += slab_specs(entry[1])
        operands += [entry[0]]
    in_specs += [line] * 4 + [tile_of(far_k[1]), tile_of(far_v[1])]
    operands += [p.reshape(p.shape[0], 1, width) for p in params] + [far_k[0], far_v[0]]
    aliases = {}
    out_tile = pl.BlockSpec((tokens, block), lambda i, f: (0, i))
    out = jax.ShapeDtypeStruct((tokens, width), jnp.bfloat16)
    count = 3 if keep_kv else 1
    out_shapes = (out,) * count
    out_specs = (out_tile,) * count
    if query_rows is not None:
        assert not keep_kv and entry is None
        out_shapes = (jax.ShapeDtypeStruct((query_rows, width), jnp.bfloat16),)
        out_specs = (pl.BlockSpec((query_rows, block), lambda i, f: (0, i)),)
    if into is not None:
        assert query_rows is not None
        buffer, slot = into
        in_specs.append(pl.BlockSpec(memory_space=pl.ANY))
        operands.append(buffer)
        aliases = {len(operands): 0}
        out_shapes = (jax.ShapeDtypeStruct(buffer.shape, buffer.dtype),)
        out_specs = (pl.BlockSpec((None, query_rows, block), lambda i, f: (slot, 0, i)),)
    if emit_rows is not None:
        half, rows, slots = emit_rows
        out_shapes += (
            jax.ShapeDtypeStruct((half, width), jnp.bfloat16),
            jax.ShapeDtypeStruct((slots, rows, width), jnp.bfloat16),
        )
        out_specs += (
            pl.BlockSpec((half, block), lambda i, f: (0, i)),
            pl.BlockSpec((None, rows, block), lambda i, f: (0, 0, i)),
        )
    return pl.pallas_call(
        functools.partial(
            layer_kernel,
            two_sources=entry is not None,
            keep_kv=keep_kv,
            query_rows=query_rows,
            emit_rows=emit_rows is not None,
            aliased=into is not None,
            halves=halves,
        ),
        out_shape=out_shapes,
        grid_spec=pltpu.PrefetchScalarGridSpec(
            num_scalar_prefetch=1,
            grid=(width // block,),
            in_specs=in_specs,
            out_specs=out_specs,
        ),
        input_output_aliases=aliases,
        cost_estimate=pl.CostEstimate(
            flops=8 * tokens * 2 * tokens * width,
            transcendentals=tokens * 2 * tokens * (width // HD),
            bytes_accessed=(4 + 2 * count) * tokens * width,
        ),
    )(flags, *operands)


def per_device(
    perturbed_frame_activation,
    inbound_activation,
    section_block_indices,
    tile_arrival_permutation,
    adaptive_shifting,
    adaptive_scaling,
    tier_query_factor,
    tier_skip_coefficient,
    earlier_step_lookup_matrix,
    earlier_step_content_matrix,
):
    segment = lax.axis_index("segment")
    place = lax.axis_index("ctx")
    patch_count = tile_arrival_permutation.shape[0]
    rows = inbound_activation.shape[1]
    width = inbound_activation.shape[2]
    slot_count = earlier_step_lookup_matrix.shape[1]
    layers_here = section_block_indices[0]

    def pick_patch(stack, patch, axis):
        chosen = lax.index_in_dim(stack, 0, axis, keepdims=False)
        for other in range(1, stack.shape[axis]):
            chosen = jnp.where(patch == other, lax.index_in_dim(stack, other, axis, keepdims=False), chosen)
        return chosen

    def arrival(position):
        chosen = tile_arrival_permutation[0]
        for index in range(1, patch_count):
            chosen = jnp.where(position == index, tile_arrival_permutation[index], chosen)
        return chosen

    first_rows = jnp.where(
        segment == 0,
        pick_patch(perturbed_frame_activation, tile_arrival_permutation[0], 0),
        inbound_activation[0],
    )
    entry_rows = [first_rows[None]]
    for turn in range(1, patch_count):
        entry_rows.append(pick_patch(perturbed_frame_activation, tile_arrival_permutation[turn], 0)[None])
    other_patch = arrival(jnp.mod(1 - segment, patch_count))
    candidates = [
        jnp.concatenate(
            entry_rows
            + [earlier_step_lookup_matrix[0, :, patch], earlier_step_content_matrix[0, :, patch]],
            axis=0,
        )
        for patch in range(patch_count)
    ]
    packed = candidates[0]
    for patch in range(1, patch_count):
        packed = jnp.where(other_patch == patch, candidates[patch], packed)
    whole = lax.all_gather(packed, "ctx", axis=1, tiled=True)
    params = [
        adaptive_shifting[0],
        adaptive_scaling[0],
        tier_query_factor[0],
        tier_skip_coefficient[0],
    ]
    first_segment = (segment == 0).astype(jnp.int32)
    core = jnp.mod(place, 2)
    half = rows * lax.axis_size("ctx") // 2

    def flags(tier):
        live = (layers_here > tier).astype(jnp.int32)
        return jnp.stack([live, first_segment, (place * rows).astype(jnp.int32), (core * half).astype(jnp.int32)])

    source = (whole, 0)
    turn_zero_kv = []
    for tier in range(slot_count):
        last = tier == slot_count - 1
        results = fused_layer(
            flags(tier),
            source,
            params,
            tier,
            (whole, patch_count + tier),
            (whole, patch_count + slot_count + tier),
            emit_rows=(half, rows, patch_count) if last else None,
        )
        state, fresh_key, fresh_value = results[:3]
        source = (state[None], 0)
        turn_zero_kv.append(((fresh_key[None], 0), (fresh_value[None], 0)))
    sent, outcomes = results[3:]
    count = lax.axis_size("segment")
    for turn in range(1, patch_count):
        pairs = [(i, i + 1) for i in range(count - 1)]
        quarter = sent.shape[0] // 2
        got = jnp.concatenate(
            [lax.ppermute(sent[:quarter], "segment", pairs), lax.ppermute(sent[quarter:], "segment", pairs)],
            axis=0,
        )
        ctx_count = lax.axis_size("ctx")
        swapped = lax.ppermute(got, "ctx", [(c, c ^ 1) for c in range(ctx_count)])
        source = [got, swapped]
        entry = (whole, turn)
        for tier in range(slot_count):
            last = tier == slot_count - 1
            if last:
                assert turn == patch_count - 1
                (outcomes,) = fused_layer(
                    flags(tier),
                    source,
                    params,
                    tier,
                    *turn_zero_kv[tier],
                    keep_kv=False,
                    query_rows=rows,
                    into=(outcomes, turn),
                )
            else:
                (state,) = fused_layer(
                    flags(tier), source, params, tier, *turn_zero_kv[tier], entry=entry, keep_kv=False
                )
                source = (state[None], 0)
                entry = None
    return outcomes[None]


def solution(mesh):
    return jax.shard_map(
        per_device,
        mesh=mesh,
        in_specs=(
            P(None, "ctx", None),
            P("segment", "ctx", None),
            P("segment"),
            P(),
            P("segment", None, None),
            P("segment", None, None),
            P("segment", None, None),
            P("segment", None, None),
            P("segment", None, None, "ctx", None),
            P("segment", None, None, "ctx", None),
        ),
        out_specs=P("segment", None, "ctx", None),
        check_vma=False,
    )
```

```python
import functools
import math

import jax
import jax.numpy as jnp
from jax import lax
from jax.experimental import pallas as pl
from jax.experimental.pallas import tpu as pltpu
from jax.sharding import PartitionSpec as P

HD = 128
EPSILON = 1e-06


def head_norm(values):
    return values * lax.rsqrt(jnp.mean(values * values, axis=-1, keepdims=True) + EPSILON)


def layer_kernel(flags_ref, *refs, two_sources, keep_kv, query_rows, emit_rows, aliased, halves):
    if halves:
        received_ref, partner_ref, *refs = refs
        received_first = flags_ref[3] == 0
        received, partner = received_ref[...], partner_ref[...]
        arrived = jnp.concatenate(
            [jnp.where(received_first, received, partner), jnp.where(received_first, partner, received)],
            axis=0,
        )
    else:
        full_ref, *refs = refs
        x_ref = full_ref
    if two_sources:
        entry_full_ref, *refs = refs
        entry_x_ref = entry_full_ref
    shift_ref, stretch_ref, factor_ref, skip_ref, kf_ref, vf_ref, *refs = refs
    if aliased:
        refs = refs[1:]
    o_ref, *refs = refs
    kv_refs = refs[:2] if keep_kv else ()
    live = flags_ref[0] > 0
    scale = 1.0 / math.sqrt(HD)
    dims = (((1,), (1,)), ((), ()))
    if halves:
        assert query_rows is None
        whole = state = arrived
    else:
        whole = full_ref[...]
        state = x_ref[...]
    if two_sources:
        use_entry = flags_ref[1] > 0
        whole = jnp.where(use_entry, entry_full_ref[...], whole)
        state = jnp.where(use_entry, entry_x_ref[...], state)
    def row_scale_of(rows_value):
        rows_value = rows_value.astype(jnp.float32)
        return lax.rsqrt(jnp.mean(rows_value * rows_value, axis=-1, keepdims=True) + EPSILON)

    row_scale = row_scale_of(whole)
    if query_rows is None:
        state_q, row_scale_q = state, row_scale
    else:
        start = pl.multiple_of(flags_ref[2], query_rows)
        state_q = x_ref[pl.ds(start, query_rows), :]
        row_scale_q = row_scale_of(full_ref[pl.ds(start, query_rows), :])
    for j in range(state.shape[1] // HD):
        cols = slice(j * HD, (j + 1) * HD)
        stretch = 1.0 + stretch_ref[:, cols]
        x_all = state[:, cols].astype(jnp.float32)
        hidden = x_all * row_scale * stretch + shift_ref[:, cols]
        fresh_key = head_norm(hidden * factor_ref[:, cols]).astype(jnp.bfloat16)
        fresh_value = hidden.astype(jnp.bfloat16)
        x_rounded = state_q[:, cols]
        x = x_rounded.astype(jnp.float32)
        if query_rows is not None:
            hidden = x * row_scale_q * stretch + shift_ref[:, cols]
        query = head_norm(hidden).astype(jnp.bfloat16)
        if keep_kv:
            kv_refs[0][:, cols] = fresh_key
            kv_refs[1][:, cols] = fresh_value
        keys = jnp.concatenate([fresh_key, kf_ref[:, cols]], axis=0)
        values = jnp.concatenate([fresh_value, vf_ref[:, cols]], axis=0)
        weights = jnp.exp(lax.dot_general(query, keys, dims, preferred_element_type=jnp.float32) * scale)
        total = jnp.sum(weights, axis=-1, keepdims=True)
        numerator = jnp.dot(weights.astype(jnp.bfloat16), values, preferred_element_type=jnp.float32)
        attended = numerator / total
        new_state = (x + skip_ref[:, cols] * attended).astype(o_ref.dtype)
        o_ref[:, cols] = jnp.where(live, new_state, x_rounded)
    if emit_rows:
        half_ref, rows_ref = refs[len(kv_refs) :]
        half = half_ref.shape[0]
        rows = rows_ref.shape[0]
        half_ref[...] = o_ref[pl.ds(pl.multiple_of(flags_ref[3], half), half), :]
        rows_ref[...] = o_ref[pl.ds(pl.multiple_of(flags_ref[2], rows), rows), :]


def fused_layer(
    flags,
    source,
    params,
    tier,
    far_k,
    far_v,
    entry=None,
    keep_kv=True,
    query_rows=None,
    emit_rows=None,
    into=None,
):
    halves = isinstance(source, list)
    if halves:
        tokens = source[0].shape[0] * 2
        width = source[0].shape[1]
    else:
        array, slab = source
        _, tokens, width = array.shape
    block = width

    def slab_specs(slab_index):
        return [pl.BlockSpec((None, tokens, width), lambda i, f: (slab_index, 0, 0))]

    def tile_of(slab_index):
        return pl.BlockSpec((None, tokens, block), lambda i, f: (slab_index, 0, i))

    line = pl.BlockSpec((None, 1, block), lambda i, f: (tier, 0, i))
    if halves:
        in_specs = [pl.BlockSpec((tokens // 2, width), lambda i, f: (0, 0))] * 2
        operands = list(source)
    else:
        in_specs = slab_specs(slab)
        operands = [array]
    if entry is not None:
        in_specs += slab_specs(entry[1])
        operands += [entry[0]]
    in_specs += [line] * 4 + [tile_of(far_k[1]), tile_of(far_v[1])]
    operands += [p.reshape(p.shape[0], 1, width) for p in params] + [far_k[0], far_v[0]]
    aliases = {}
    out_tile = pl.BlockSpec((tokens, block), lambda i, f: (0, i))
    out = jax.ShapeDtypeStruct((tokens, width), jnp.bfloat16)
    count = 3 if keep_kv else 1
    out_shapes = (out,) * count
    out_specs = (out_tile,) * count
    if query_rows is not None:
        assert not keep_kv and entry is None
        out_shapes = (jax.ShapeDtypeStruct((query_rows, width), jnp.bfloat16),)
        out_specs = (pl.BlockSpec((query_rows, block), lambda i, f: (0, i)),)
    if into is not None:
        assert query_rows is not None
        buffer, slot = into
        in_specs.append(pl.BlockSpec(memory_space=pl.ANY))
        operands.append(buffer)
        aliases = {len(operands): 0}
        out_shapes = (jax.ShapeDtypeStruct(buffer.shape, buffer.dtype),)
        out_specs = (pl.BlockSpec((None, query_rows, block), lambda i, f: (slot, 0, i)),)
    if emit_rows is not None:
        half, rows, slots = emit_rows
        out_shapes += (
            jax.ShapeDtypeStruct((half, width), jnp.bfloat16),
            jax.ShapeDtypeStruct((slots, rows, width), jnp.bfloat16),
        )
        out_specs += (
            pl.BlockSpec((half, block), lambda i, f: (0, i)),
            pl.BlockSpec((None, rows, block), lambda i, f: (0, 0, i)),
        )
    return pl.pallas_call(
        functools.partial(
            layer_kernel,
            two_sources=entry is not None,
            keep_kv=keep_kv,
            query_rows=query_rows,
            emit_rows=emit_rows is not None,
            aliased=into is not None,
            halves=halves,
        ),
        out_shape=out_shapes,
        grid_spec=pltpu.PrefetchScalarGridSpec(
            num_scalar_prefetch=1,
            grid=(width // block,),
            in_specs=in_specs,
            out_specs=out_specs,
        ),
        input_output_aliases=aliases,
        cost_estimate=pl.CostEstimate(
            flops=8 * tokens * 2 * tokens * width,
            transcendentals=tokens * 2 * tokens * (width // HD),
            bytes_accessed=(4 + 2 * count) * tokens * width,
        ),
    )(flags, *operands)


def per_device(
    perturbed_frame_activation,
    inbound_activation,
    section_block_indices,
    tile_arrival_permutation,
    adaptive_shifting,
    adaptive_scaling,
    tier_query_factor,
    tier_skip_coefficient,
    earlier_step_lookup_matrix,
    earlier_step_content_matrix,
):
    segment = lax.axis_index("segment")
    place = lax.axis_index("ctx")
    patch_count = tile_arrival_permutation.shape[0]
    rows = inbound_activation.shape[1]
    width = inbound_activation.shape[2]
    slot_count = earlier_step_lookup_matrix.shape[1]
    layers_here = section_block_indices[0]

    def pick_patch(stack, patch, axis):
        chosen = lax.index_in_dim(stack, 0, axis, keepdims=False)
        for other in range(1, stack.shape[axis]):
            chosen = jnp.where(patch == other, lax.index_in_dim(stack, other, axis, keepdims=False), chosen)
        return chosen

    def arrival(position):
        chosen = tile_arrival_permutation[0]
        for index in range(1, patch_count):
            chosen = jnp.where(position == index, tile_arrival_permutation[index], chosen)
        return chosen

    first_rows = jnp.where(
        segment == 0,
        pick_patch(perturbed_frame_activation, tile_arrival_permutation[0], 0),
        inbound_activation[0],
    )
    entry_rows = [first_rows[None]]
    for turn in range(1, patch_count):
        entry_rows.append(pick_patch(perturbed_frame_activation, tile_arrival_permutation[turn], 0)[None])
    other_patch = arrival(jnp.mod(1 - segment, patch_count))
    candidates = [
        jnp.concatenate(
            entry_rows
            + [earlier_step_lookup_matrix[0, :, patch], earlier_step_content_matrix[0, :, patch]],
            axis=0,
        )
        for patch in range(patch_count)
    ]
    packed = candidates[0]
    for patch in range(1, patch_count):
        packed = jnp.where(other_patch == patch, candidates[patch], packed)
    whole = lax.all_gather(packed, "ctx", axis=1, tiled=True)
    params = [
        adaptive_shifting[0],
        adaptive_scaling[0],
        tier_query_factor[0],
        tier_skip_coefficient[0],
    ]
    first_segment = (segment == 0).astype(jnp.int32)
    core = jnp.mod(place, 2)
    half = rows * lax.axis_size("ctx") // 2

    def flags(tier):
        live = (layers_here > tier).astype(jnp.int32)
        return jnp.stack([live, first_segment, (place * rows).astype(jnp.int32), (core * half).astype(jnp.int32)])

    source = (whole, 0)
    turn_zero_kv = []
    for tier in range(slot_count):
        last = tier == slot_count - 1
        results = fused_layer(
            flags(tier),
            source,
            params,
            tier,
            (whole, patch_count + tier),
            (whole, patch_count + slot_count + tier),
            emit_rows=(half, rows, patch_count) if last else None,
        )
        state, fresh_key, fresh_value = results[:3]
        source = (state[None], 0)
        turn_zero_kv.append(((fresh_key[None], 0), (fresh_value[None], 0)))
    sent, outcomes = results[3:]
    count = lax.axis_size("segment")
    for turn in range(1, patch_count):
        got = lax.ppermute(sent, "segment", [(i, i + 1) for i in range(count - 1)])
        ctx_count = lax.axis_size("ctx")
        swapped = lax.ppermute(got, "ctx", [(c, c ^ 1) for c in range(ctx_count)])
        source = [got, swapped]
        entry = (whole, turn)
        for tier in range(slot_count):
            last = tier == slot_count - 1
            if last:
                assert turn == patch_count - 1
                (outcomes,) = fused_layer(
                    flags(tier),
                    source,
                    params,
                    tier,
                    *turn_zero_kv[tier],
                    keep_kv=False,
                    query_rows=rows,
                    into=(outcomes, turn),
                )
            else:
                (state,) = fused_layer(
                    flags(tier), source, params, tier, *turn_zero_kv[tier], entry=entry, keep_kv=False
                )
                source = (state[None], 0)
                entry = None
    return outcomes[None]


def solution(mesh):
    return jax.shard_map(
        per_device,
        mesh=mesh,
        in_specs=(
            P(None, "ctx", None),
            P("segment", "ctx", None),
            P("segment"),
            P(),
            P("segment", None, None),
            P("segment", None, None),
            P("segment", None, None),
            P("segment", None, None),
            P("segment", None, None, "ctx", None),
            P("segment", None, None, "ctx", None),
        ),
        out_specs=P("segment", None, "ctx", None),
        check_vma=False,
    )
```
